128 devices in a mesh: ctx: 16 (over x, z_lo, core), tp: 8 (over z_hi, y).
Axes of the slice: x: 4, y: 4, z: 4 (z_hi: 2, z_lo: 2; z = z_hi * 2 + z_lo), core: 2. Of those that a mesh axis runs over, the one named last changes fastest.
Arguments:
- queries: bfloat16 [16384, 8192], P(('ctx', 'tp')), may hold values from -48 to 48
- key_rows: bfloat16 [16384, 1024], P('ctx', 'tp'), may hold values from -8 to 8
- value_rows: bfloat16 [16384, 1024], P('ctx', 'tp'), may hold values from -6 to 6
- out_grad: bfloat16 [16384, 8192], P(('ctx', 'tp')), may hold values from -6 to 6
- doc_ids: int32 [16384], replicated, may hold values from 0 to 31, never falling along the last dimension, each value on 1 to 1408 neighbouring positions
- block_owner: int32 [128], replicated, may hold values from 0 to 15, as said below
Outputs:
- attended: bfloat16 [16384, 8192], P('ctx', 'tp')
- query_grad: bfloat16 [16384, 8192], P('ctx', 'tp')
- key_grad: bfloat16 [16384, 1024], P('ctx', 'tp')
- value_grad: bfloat16 [16384, 1024], P('ctx', 'tp')
The draws below stay inside these ranges and needn't reach their ends.
Inputs may be any that keep to these rules, and one draw needn't show every extreme that they name: `doc_ids`: ids never fall along the sequence; every document has 1 to 1408 tokens and one has exactly 1408. `block_owner`: every context shard takes exactly 8 blocks, and at most one of the blocks s * 8 to (s + 1) * 8 - 1 of any index s.
All inputs are finite; a program needn't handle non-finite values.
Results may differ from the reference program's by a relative error of at most 0.012.
The reference program's roundings to bfloat16 on the way (of `soft_low`, `natural_out` and `score_grad`) count: a program that leaves them out, or rounds other values in their place, can miss the bound.
Values may be sent and summed in bfloat16 or wider, within the bound.
No kernel may reach another device: no remote copies, remote signals or barrier semaphores. Data moves between devices by JAX's collectives and lax.ppermute only.
A program may use at most 128 MiB of HBM per device.

```python
import math
import jax
import jax.numpy as jnp
import numpy as np
from jax import lax

HEADS = 64
KV_HEADS = 8
HEAD_DIM = 128
BLOCK = 128
BAND = 12
TOKENS = 16384
BLOCKS = 128
BLK_DEV = 8
DOC_MOST = 1408
DOCS = 32
N_CTX = 16


def paired_rows(key):
    base_key = jax.random.fold_in(key, 7)
    key_a, key_b = jax.random.split(base_key, 2)
    group = HEADS // KV_HEADS
    key_main = jnp.clip(jax.random.normal(key_a, (TOKENS, KV_HEADS, HEAD_DIM), jnp.float32), -4.0, 4.0)
    query_main = jnp.clip(jax.random.normal(key_b, (TOKENS, KV_HEADS, group, HEAD_DIM), jnp.float32), -4.0, 4.0)
    key_out = key_main
    query_out = query_main
    return (query_out.reshape(TOKENS, HEADS * HEAD_DIM), key_out.reshape(TOKENS, KV_HEADS * HEAD_DIM))


def draw_queries(key, part):
    return paired_rows(key)[0].astype(jnp.bfloat16)


def draw_key_rows(key, part):
    return paired_rows(key)[1].astype(jnp.bfloat16)


def draw_block_owner(key, part):
    base_key = jax.random.fold_in(key, 5)
    key_a, key_b, key_c = jax.random.split(base_key, 3)
    offsets = jax.random.permutation(key_a, N_CTX)[:BLK_DEV]
    relabel = jax.random.permutation(key_b, N_CTX)
    shuffle = jax.random.permutation(key_c, N_CTX)
    target_grid = (shuffle[:, None] + offsets[None, :]) % N_CTX
    return relabel[target_grid].reshape(N_CTX * BLK_DEV).astype(jnp.int32)


def block_scale(stream_key, dims, pieces, low, largest):
    def one(dim, blocks):
        heights = jax.random.uniform(jax.random.fold_in(jax.random.fold_in(stream_key, 6), dim), (blocks,), jnp.float32, low / len(pieces), largest / len(pieces))
        return jnp.repeat(jnp.exp(heights), dims[dim] // blocks).reshape((-1,) + (1,) * (len(dims) - dim - 1))

    factor_of = one(*pieces[0])
    for cut in pieces[1:]:
        factor_of = factor_of * one(*cut)
    return factor_of


def split_up(amount, total, most, lean):
    loads = [(1 << 20) // math.isqrt(standing ** lean) + 1 for standing in range(2, amount + 1)]
    rest, holding = total - most - (amount - 1), [1] * (amount - 1)
    while rest > 0:
        movable = [i for i in range(amount - 1) if holding[i] < most]
        pool, left = sum([loads[i] for i in movable]), rest
        for i in movable:
            addition = min(most - holding[i], max(1, left * loads[i] // pool), rest)
            holding[i] = holding[i] + addition
            rest = rest - addition
    return np.array([most] + holding)


def ragged(own_key, number_of, total, reach, lean):
    if number_of == 2:
        one = jax.random.randint(own_key, (), max(1, total - reach), min(reach, total - 1) + 1)
        return jnp.stack([one, total - one])
    lengths = jnp.asarray(split_up(number_of, total, reach, lean), jnp.int32)
    couples = (number_of - 1) // 2
    donor, sink = lengths[1:1 + 2 * couples:2], lengths[2:2 + 2 * couples:2]
    margin = jnp.minimum(donor - 1, reach - sink)
    moved = jax.random.randint(jax.random.fold_in(own_key, 1), (couples,), 0, 1 << 20) % (margin + 1)
    lengths = lengths.at[1:1 + 2 * couples:2].set(donor - moved).at[2:2 + 2 * couples:2].set(sink + moved)
    return lengths[jax.random.permutation(jax.random.fold_in(own_key, 2), number_of)]


def noise(own_key, dims, scale, limit, cuts=(), kind=jnp.bfloat16):
    factor_of = block_scale(own_key, dims, cuts, -0.22, 0.18) if cuts else 1.0
    result = jax.random.normal(own_key, dims, jnp.float32) * scale * factor_of
    return jnp.minimum(jnp.maximum(result, -limit), limit).astype(kind)


def setup_inputs(seed: int = 0) -> dict:
    keys = jax.random.split(jax.random.key(seed), 7)
    queries = draw_queries(jax.random.fold_in(keys[6], 71), 0)
    key_rows = draw_key_rows(jax.random.fold_in(keys[6], 71), 0)
    value_rows = noise(keys[2], (TOKENS, KV_HEADS * HEAD_DIM), 1.0, 6.0, ((0, 16), (1, 8)))
    out_grad = noise(keys[3], (TOKENS, HEADS * HEAD_DIM), 1.0, 6.0, ((0, 128),))
    doc_ids = jnp.searchsorted(jnp.cumsum(ragged(keys[4], DOCS, TOKENS, DOC_MOST, 2)), jnp.arange(TOKENS), side="right").astype(jnp.int32)
    block_owner = draw_block_owner(jax.random.fold_in(keys[6], 71), 0)
    return {"queries": queries, "key_rows": key_rows, "value_rows": value_rows, "out_grad": out_grad, "doc_ids": doc_ids, "block_owner": block_owner}


def lift_float(values_low):
    return lax.optimization_barrier(values_low).astype(jnp.float32)


def window_of(key_rows, value_rows, block_id):
    window_rows = BAND * BLOCK
    window_start = (jnp.maximum(block_id - BAND + 1, 0) * BLOCK).astype(jnp.int32)
    key_window = lax.dynamic_slice_in_dim(key_rows, window_start, window_rows, 0)
    value_window = lax.dynamic_slice_in_dim(value_rows, window_start, window_rows, 0)
    key_window = key_window.astype(jnp.float32).reshape(window_rows, KV_HEADS, HEAD_DIM)
    value_window = value_window.astype(jnp.float32).reshape(window_rows, KV_HEADS, HEAD_DIM)
    return window_start, key_window, value_window


def scores_for(query_block, key_window, block_id, window_start, doc_ids):
    window_rows = key_window.shape[0]
    query_heads = query_block.astype(jnp.float32).reshape(BLOCK, KV_HEADS, HEADS // KV_HEADS, HEAD_DIM)
    raw_scores = jnp.einsum("qkgd,wkd->kgqw", query_heads, key_window) * (HEAD_DIM ** -0.5)
    query_start = (block_id * BLOCK).astype(jnp.int32)
    query_pos = query_start + jnp.arange(BLOCK, dtype=jnp.int32)
    key_pos = window_start + jnp.arange(window_rows, dtype=jnp.int32)
    query_doc = lax.dynamic_slice_in_dim(doc_ids, query_start, BLOCK, 0)
    key_doc = lax.dynamic_slice_in_dim(doc_ids, window_start, window_rows, 0)
    allowed = (query_doc[:, None] == key_doc[None, :]) & (key_pos[None, :] <= query_pos[:, None])
    return jnp.where(allowed[None, None], raw_scores, -1e30), query_heads


def reference(queries, key_rows, value_rows, out_grad, doc_ids, block_owner):
    inv_root = HEAD_DIM ** -0.5
    window_rows = BAND * BLOCK
    block_ids = jnp.arange(BLOCKS, dtype=jnp.int32)
    query_blocks = queries.reshape(BLOCKS, BLOCK, HEADS * HEAD_DIM)
    grad_blocks = out_grad.reshape(BLOCKS, BLOCK, HEADS * HEAD_DIM)

    def forward(running, inputs):
        query_block, block_id = inputs
        window_start, key_window, value_window = window_of(key_rows, value_rows, block_id)
        scores, _ = scores_for(query_block, key_window, block_id, window_start, doc_ids)
        row_max = jnp.max(scores, axis=-1, keepdims=True)
        log_total = row_max + jnp.log(jnp.sum(jnp.exp(scores - row_max), axis=-1, keepdims=True))
        soft_low = jnp.exp(scores - log_total).astype(jnp.bfloat16)
        natural_out = jnp.einsum("kgqw,wkd->qkgd", lift_float(soft_low), value_window)
        return running, (natural_out.reshape(BLOCK, HEADS * HEAD_DIM).astype(jnp.bfloat16), log_total)

    _, (out_blocks, log_totals) = lax.scan(forward, jnp.zeros((), jnp.float32), (query_blocks, block_ids))

    def backward(running, inputs):
        key_grad, value_grad = running
        query_block, grad_block, out_block, log_total, block_id = inputs
        window_start, key_window, value_window = window_of(key_rows, value_rows, block_id)
        scores, query_heads = scores_for(query_block, key_window, block_id, window_start, doc_ids)
        grad_heads = grad_block.astype(jnp.float32).reshape(query_heads.shape)
        out_heads = out_block.astype(jnp.float32).reshape(query_heads.shape)
        weights = jnp.exp(scores - log_total)
        soft_low = lift_float(weights.astype(jnp.bfloat16))
        row_dot = jnp.transpose(jnp.sum(grad_heads * out_heads, axis=-1), (1, 2, 0))[..., None]
        prob_grad = jnp.einsum("qkgd,wkd->kgqw", grad_heads, value_window)
        score_grad = lift_float((weights * (prob_grad - row_dot)).astype(jnp.bfloat16))
        query_part = jnp.einsum("kgqw,wkd->qkgd", score_grad, key_window) * inv_root
        key_part = jnp.einsum("kgqw,qkgd->wkd", score_grad, query_heads) * inv_root
        value_part = jnp.einsum("kgqw,qkgd->wkd", soft_low, grad_heads)
        old_keys = lax.dynamic_slice_in_dim(key_grad, window_start, window_rows, 0)
        old_values = lax.dynamic_slice_in_dim(value_grad, window_start, window_rows, 0)
        key_grad = lax.dynamic_update_slice_in_dim(key_grad, old_keys + key_part.reshape(window_rows, -1), window_start, 0)
        value_grad = lax.dynamic_update_slice_in_dim(value_grad, old_values + value_part.reshape(window_rows, -1), window_start, 0)
        return (key_grad, value_grad), query_part.reshape(BLOCK, HEADS * HEAD_DIM).astype(jnp.bfloat16)

    zero_grads = (jnp.zeros(key_rows.shape, jnp.float32), jnp.zeros(value_rows.shape, jnp.float32))
    (key_grad, value_grad), dq_blocks = lax.scan(
        backward, zero_grads, (query_blocks, grad_blocks, out_blocks, log_totals, block_ids))
    context_order = jnp.argsort(block_owner * BLOCKS + block_ids).astype(jnp.int32)
    attended = out_blocks[context_order].reshape(TOKENS, HEADS * HEAD_DIM)
    query_grad = dq_blocks[context_order].reshape(TOKENS, HEADS * HEAD_DIM)
    return attended, query_grad, key_grad.astype(jnp.bfloat16), value_grad.astype(jnp.bfloat16)
```

```python
import jax
import jax.numpy as jnp
from jax import lax
from jax.sharding import PartitionSpec as P

HEADS = 64
KV_HEADS = 8
HEAD_DIM = 128
BLOCK = 128
BAND = 12


def routing(block_owner, ctx_count, ctx_rank, blocks_here):
    owner_grid = block_owner.reshape(ctx_count, blocks_here)
    own_targets = lax.dynamic_index_in_dim(owner_grid, ctx_rank, 0, keepdims=False)
    targets = jnp.arange(ctx_count, dtype=jnp.int32)
    send_pick = (own_targets[None, :] == targets[:, None]).astype(jnp.bfloat16)
    arrivals = (owner_grid == ctx_rank).astype(jnp.int32)
    present = jnp.sum(arrivals, axis=1)
    arrival_rank = jnp.cumsum(present) - 1
    slot_index = jnp.arange(blocks_here, dtype=jnp.int32)
    chosen = (present[None, :] == 1) & (arrival_rank[None, :] == slot_index[:, None])
    source_block = targets * blocks_here + jnp.sum(arrivals * slot_index[None, :], axis=1)
    held_ids = jnp.sum(chosen.astype(jnp.int32) * source_block[None, :], axis=1)
    return (send_pick, chosen.astype(jnp.bfloat16), held_ids)


def select_rows(selector, blocks):
    picked = jnp.einsum("ab,brh->arh", selector, blocks, preferred_element_type=jnp.float32)
    return picked.astype(jnp.bfloat16)


def halo_docs(doc_ids, first_row, halo_rows):
    positions = first_row + jnp.arange(halo_rows, dtype=jnp.int32)
    picked = jnp.take(doc_ids, jnp.clip(positions, 0, doc_ids.shape[0] - 1), axis=0)
    return jnp.where(positions >= 0, picked, -1)


def masked_scores(query_block, key_window, query_doc, key_doc, local_block):
    window_rows = key_window.shape[0]
    kv_local = key_window.shape[1]
    query_heads = query_block.reshape(BLOCK, kv_local, HEADS // KV_HEADS, HEAD_DIM)
    raw_scores = jnp.einsum(
        "qkgd,wkd->kgqw", query_heads, key_window, preferred_element_type=jnp.float32
    ) * HEAD_DIM ** (-0.5)
    query_pos = (BAND - 1) * BLOCK + jnp.arange(BLOCK, dtype=jnp.int32)
    key_pos = jnp.arange(window_rows, dtype=jnp.int32)
    allowed = (query_doc[:, None] == key_doc[None, :]) & (key_pos[None, :] <= query_pos[:, None])
    return (jnp.where(allowed[None, None], raw_scores, -1e30), query_heads)


def window_of(halo_key, halo_value, halo_doc, local_block):
    window_rows = BAND * BLOCK
    kv_local = halo_key.shape[1] // HEAD_DIM
    start = local_block * BLOCK
    key_window = lax.dynamic_slice_in_dim(halo_key, start, window_rows, 0)
    value_window = lax.dynamic_slice_in_dim(halo_value, start, window_rows, 0)
    key_doc = lax.dynamic_slice_in_dim(halo_doc, start, window_rows, 0)
    query_doc = lax.dynamic_slice_in_dim(halo_doc, start + (BAND - 1) * BLOCK, BLOCK, 0)
    return (
        key_window.reshape(window_rows, kv_local, HEAD_DIM),
        value_window.reshape(window_rows, kv_local, HEAD_DIM),
        query_doc,
        key_doc,
    )


def attend_forward(query_blocks, halo_key, halo_value, halo_doc):

    def advance(running, inputs):
        query_block, local_block = inputs
        key_window, value_window, query_doc, key_doc = window_of(
            halo_key, halo_value, halo_doc, local_block
        )
        scores, _ = masked_scores(query_block, key_window, query_doc, key_doc, local_block)
        row_max = jnp.max(scores, axis=-1, keepdims=True)
        log_total = row_max + jnp.log(jnp.sum(jnp.exp(scores - row_max), axis=-1, keepdims=True))
        soft_low = jnp.exp(scores - log_total).astype(jnp.bfloat16)
        natural_out = jnp.einsum(
            "kgqw,wkd->qkgd", soft_low, value_window, preferred_element_type=jnp.float32
        )
        return (running, (natural_out.reshape(BLOCK, -1).astype(jnp.bfloat16), log_total))

    local_ids = jnp.arange(query_blocks.shape[0], dtype=jnp.int32)
    _, (out_blocks, log_totals) = lax.scan(
        advance, jnp.zeros((), jnp.float32), (query_blocks, local_ids)
    )
    return (out_blocks, log_totals)


def attend_backward(query_blocks, grad_blocks, out_blocks, log_totals, halo_key, halo_value, halo_doc):
    window_rows = BAND * BLOCK
    inv_root = HEAD_DIM ** (-0.5)

    def advance(running, inputs):
        key_grad, value_grad = running
        query_block, grad_block, out_block, log_total, local_block = inputs
        key_window, value_window, query_doc, key_doc = window_of(
            halo_key, halo_value, halo_doc, local_block
        )
        scores, query_heads = masked_scores(
            query_block, key_window, query_doc, key_doc, local_block
        )
        grad_heads = grad_block.reshape(query_heads.shape)
        out_heads = out_block.reshape(query_heads.shape)
        weights = jnp.exp(scores - log_total)
        soft_low = weights.astype(jnp.bfloat16)
        row_dot = jnp.sum(grad_heads.astype(jnp.float32) * out_heads.astype(jnp.float32), axis=-1)
        row_dot = jnp.transpose(row_dot, (1, 2, 0))[..., None]
        prob_grad = jnp.einsum(
            "qkgd,wkd->kgqw", grad_heads, value_window, preferred_element_type=jnp.float32
        )
        score_grad = (weights * (prob_grad - row_dot)).astype(jnp.bfloat16)
        query_part = (
            jnp.einsum("kgqw,wkd->qkgd", score_grad, key_window, preferred_element_type=jnp.float32)
            * inv_root
        )
        key_part = (
            jnp.einsum(
                "kgqw,qkgd->wkd", score_grad, query_heads, preferred_element_type=jnp.float32
            )
            * inv_root
        )
        value_part = jnp.einsum(
            "kgqw,qkgd->wkd", soft_low, grad_heads, preferred_element_type=jnp.float32
        )
        start = local_block * BLOCK
        old_keys = lax.dynamic_slice_in_dim(key_grad, start, window_rows, 0)
        old_values = lax.dynamic_slice_in_dim(value_grad, start, window_rows, 0)
        key_grad = lax.dynamic_update_slice_in_dim(
            key_grad, old_keys + key_part.reshape(window_rows, -1), start, 0
        )
        value_grad = lax.dynamic_update_slice_in_dim(
            value_grad, old_values + value_part.reshape(window_rows, -1), start, 0
        )
        return ((key_grad, value_grad), query_part.reshape(BLOCK, -1).astype(jnp.bfloat16))

    zero_grads = (
        jnp.zeros(halo_key.shape, jnp.float32),
        jnp.zeros(halo_value.shape, jnp.float32),
    )
    local_ids = jnp.arange(query_blocks.shape[0], dtype=jnp.int32)
    (key_grad, value_grad), dq_blocks = lax.scan(
        advance, zero_grads, (query_blocks, grad_blocks, out_blocks, log_totals, local_ids)
    )
    return (dq_blocks, key_grad, value_grad)


def shift_from_below(x, ctx_count, distance):
    pairs = [(s, s + distance) for s in range(ctx_count - distance)]
    return lax.ppermute(x, "ctx", pairs)


def shift_to_below(x, ctx_count, distance):
    pairs = [(s + distance, s) for s in range(ctx_count - distance)]
    return lax.ppermute(x, "ctx", pairs)


def on_device(queries, key_rows, value_rows, out_grad, doc_ids, block_owner):
    ctx_count = lax.axis_size("ctx")
    tp_count = lax.axis_size("tp")
    ctx_rank = lax.axis_index("ctx")
    local_rows, width = queries.shape
    head_cols = width // tp_count
    tok_dev = key_rows.shape[0]
    kv_cols = key_rows.shape[1]
    blocks_here = tok_dev // BLOCK
    reach = (BAND - 1) * BLOCK
    far = reach - tok_dev
    send_pick, recv_pick, _ = routing(block_owner, ctx_count, ctx_rank, blocks_here)
    query_split, grad_split = (
        lax.all_to_all(
            queries.reshape(local_rows, tp_count, head_cols),
            "tp",
            split_axis=1,
            concat_axis=0,
            tiled=True,
        ),
        lax.all_to_all(
            out_grad.reshape(local_rows, tp_count, head_cols),
            "tp",
            split_axis=1,
            concat_axis=0,
            tiled=True,
        ),
    )
    query_blocks = query_split.reshape(blocks_here, BLOCK, head_cols)
    grad_blocks = grad_split.reshape(blocks_here, BLOCK, head_cols)
    kv_here = jnp.concatenate([key_rows, value_rows], axis=1)
    kv_near = shift_from_below(kv_here, ctx_count, 1)
    kv_far = shift_from_below(kv_here[tok_dev - far :], ctx_count, 2)
    halo = jnp.concatenate([kv_far, kv_near, kv_here], axis=0)
    halo_key = halo[:, :kv_cols]
    halo_value = halo[:, kv_cols:]
    halo_doc = halo_docs(doc_ids, ctx_rank * tok_dev - reach, reach + tok_dev)
    out_blocks, log_totals = attend_forward(query_blocks, halo_key, halo_value, halo_doc)
    dq_blocks, key_grad, value_grad = attend_backward(
        query_blocks, grad_blocks, out_blocks, log_totals, halo_key, halo_value, halo_doc
    )
    kv_grad = jnp.concatenate([key_grad, value_grad], axis=1)
    grad_near = shift_to_below(kv_grad[far:reach], ctx_count, 1)
    grad_far = shift_to_below(kv_grad[:far], ctx_count, 2)
    kv_total = kv_grad[reach:] + grad_near
    kv_total = kv_total.at[tok_dev - far :].add(grad_far)
    sent_out, sent_dq = (
        lax.all_to_all(
            select_rows(send_pick, out_blocks), "ctx", split_axis=0, concat_axis=0, tiled=True
        ),
        lax.all_to_all(
            select_rows(send_pick, dq_blocks), "ctx", split_axis=0, concat_axis=0, tiled=True
        ),
    )
    held_out = select_rows(recv_pick, sent_out)
    held_dq = select_rows(recv_pick, sent_dq)
    return (
        held_out.reshape(tok_dev, head_cols),
        held_dq.reshape(tok_dev, head_cols),
        kv_total[:, :kv_cols].astype(jnp.bfloat16),
        kv_total[:, kv_cols:].astype(jnp.bfloat16),
    )


def solution(mesh):
    return jax.shard_map(
        on_device,
        mesh=mesh,
        in_specs=(
            P(("ctx", "tp"), None),
            P("ctx", "tp"),
            P("ctx", "tp"),
            P(("ctx", "tp"), None),
            P(),
            P(),
        ),
        out_specs=(P("ctx", "tp"), P("ctx", "tp"), P("ctx", "tp"), P("ctx", "tp")),
        check_vma=False,
    )
```

```python
import jax
import jax.numpy as jnp
from jax import lax
from jax.sharding import PartitionSpec as P
from jax.experimental import pallas as pl
from jax.experimental.pallas import tpu as pltpu

HEADS = 64
KV_HEADS = 8
HEAD_DIM = 128
BLOCK = 128
BAND = 12


def routing(block_owner, ctx_count, ctx_rank, blocks_here):
    owner_grid = block_owner.reshape(ctx_count, blocks_here)
    own_targets = lax.dynamic_index_in_dim(owner_grid, ctx_rank, 0, keepdims=False)
    targets = jnp.arange(ctx_count, dtype=jnp.int32)
    send_pick = (own_targets[None, :] == targets[:, None]).astype(jnp.bfloat16)
    arrivals = (owner_grid == ctx_rank).astype(jnp.int32)
    present = jnp.sum(arrivals, axis=1)
    arrival_rank = jnp.cumsum(present) - 1
    slot_index = jnp.arange(blocks_here, dtype=jnp.int32)
    chosen = (present[None, :] == 1) & (arrival_rank[None, :] == slot_index[:, None])
    source_block = targets * blocks_here + jnp.sum(arrivals * slot_index[None, :], axis=1)
    held_ids = jnp.sum(chosen.astype(jnp.int32) * source_block[None, :], axis=1)
    return (send_pick, chosen.astype(jnp.bfloat16), held_ids)


def select_rows(selector, blocks):
    picked = jnp.einsum("ab,brh->arh", selector, blocks, preferred_element_type=jnp.float32)
    return picked.astype(jnp.bfloat16)


def halo_docs(doc_ids, first_row, halo_rows):
    positions = first_row + jnp.arange(halo_rows, dtype=jnp.int32)
    picked = jnp.take(doc_ids, jnp.clip(positions, 0, doc_ids.shape[0] - 1), axis=0)
    return jnp.where(positions >= 0, picked, -1)


def masked_scores(query_block, key_window, query_doc, key_doc, local_block):
    window_rows = key_window.shape[0]
    kv_local = key_window.shape[1]
    query_heads = query_block.reshape(BLOCK, kv_local, HEADS // KV_HEADS, HEAD_DIM)
    raw_scores = jnp.einsum(
        "qkgd,wkd->kgqw", query_heads, key_window, preferred_element_type=jnp.float32
    ) * HEAD_DIM ** (-0.5)
    query_pos = (BAND - 1) * BLOCK + jnp.arange(BLOCK, dtype=jnp.int32)
    key_pos = jnp.arange(window_rows, dtype=jnp.int32)
    allowed = (query_doc[:, None] == key_doc[None, :]) & (key_pos[None, :] <= query_pos[:, None])
    return (jnp.where(allowed[None, None], raw_scores, -1e30), query_heads)


def window_of(halo_key, halo_value, halo_doc, local_block):
    window_rows = BAND * BLOCK
    kv_local = halo_key.shape[1] // HEAD_DIM
    start = local_block * BLOCK
    key_window = lax.dynamic_slice_in_dim(halo_key, start, window_rows, 0)
    value_window = lax.dynamic_slice_in_dim(halo_value, start, window_rows, 0)
    key_doc = lax.dynamic_slice_in_dim(halo_doc, start, window_rows, 0)
    query_doc = lax.dynamic_slice_in_dim(halo_doc, start + (BAND - 1) * BLOCK, BLOCK, 0)
    return (
        key_window.reshape(window_rows, kv_local, HEAD_DIM),
        value_window.reshape(window_rows, kv_local, HEAD_DIM),
        query_doc,
        key_doc,
    )


def attend_forward(query_blocks, halo_key, halo_value, halo_doc):

    def advance(running, inputs):
        query_block, local_block = inputs
        key_window, value_window, query_doc, key_doc = window_of(
            halo_key, halo_value, halo_doc, local_block
        )
        scores, _ = masked_scores(query_block, key_window, query_doc, key_doc, local_block)
        row_max = jnp.max(scores, axis=-1, keepdims=True)
        log_total = row_max + jnp.log(jnp.sum(jnp.exp(scores - row_max), axis=-1, keepdims=True))
        soft_low = jnp.exp(scores - log_total).astype(jnp.bfloat16)
        natural_out = jnp.einsum(
            "kgqw,wkd->qkgd", soft_low, value_window, preferred_element_type=jnp.float32
        )
        return (running, (natural_out.reshape(BLOCK, -1).astype(jnp.bfloat16), log_total))

    local_ids = jnp.arange(query_blocks.shape[0], dtype=jnp.int32)
    _, (out_blocks, log_totals) = lax.scan(
        advance, jnp.zeros((), jnp.float32), (query_blocks, local_ids)
    )
    return (out_blocks, log_totals)


def attend_backward(query_blocks, grad_blocks, out_blocks, log_totals, halo_key, halo_value, halo_doc):
    window_rows = BAND * BLOCK
    inv_root = HEAD_DIM ** (-0.5)

    def advance(running, inputs):
        key_grad, value_grad = running
        query_block, grad_block, out_block, log_total, local_block = inputs
        key_window, value_window, query_doc, key_doc = window_of(
            halo_key, halo_value, halo_doc, local_block
        )
        scores, query_heads = masked_scores(
            query_block, key_window, query_doc, key_doc, local_block
        )
        grad_heads = grad_block.reshape(query_heads.shape)
        out_heads = out_block.reshape(query_heads.shape)
        weights = jnp.exp(scores - log_total)
        soft_low = weights.astype(jnp.bfloat16)
        row_dot = jnp.sum(grad_heads.astype(jnp.float32) * out_heads.astype(jnp.float32), axis=-1)
        row_dot = jnp.transpose(row_dot, (1, 2, 0))[..., None]
        prob_grad = jnp.einsum(
            "qkgd,wkd->kgqw", grad_heads, value_window, preferred_element_type=jnp.float32
        )
        score_grad = (weights * (prob_grad - row_dot)).astype(jnp.bfloat16)
        query_part = (
            jnp.einsum("kgqw,wkd->qkgd", score_grad, key_window, preferred_element_type=jnp.float32)
            * inv_root
        )
        key_part = (
            jnp.einsum(
                "kgqw,qkgd->wkd", score_grad, query_heads, preferred_element_type=jnp.float32
            )
            * inv_root
        )
        value_part = jnp.einsum(
            "kgqw,qkgd->wkd", soft_low, grad_heads, preferred_element_type=jnp.float32
        )
        start = local_block * BLOCK
        old_keys = lax.dynamic_slice_in_dim(key_grad, start, window_rows, 0)
        old_values = lax.dynamic_slice_in_dim(value_grad, start, window_rows, 0)
        key_grad = lax.dynamic_update_slice_in_dim(
            key_grad, old_keys + key_part.reshape(window_rows, -1), start, 0
        )
        value_grad = lax.dynamic_update_slice_in_dim(
            value_grad, old_values + value_part.reshape(window_rows, -1), start, 0
        )
        return ((key_grad, value_grad), query_part.reshape(BLOCK, -1).astype(jnp.bfloat16))

    zero_grads = (
        jnp.zeros(halo_key.shape, jnp.float32),
        jnp.zeros(halo_value.shape, jnp.float32),
    )
    local_ids = jnp.arange(query_blocks.shape[0], dtype=jnp.int32)
    (key_grad, value_grad), dq_blocks = lax.scan(
        advance, zero_grads, (query_blocks, grad_blocks, out_blocks, log_totals, local_ids)
    )
    return (dq_blocks, key_grad, value_grad)


TRANS_B = (((1,), (1,)), ((), ()))
TRANS_A = (((0,), (0,)), ((), ()))


def fused_kernel(qdoc_ref, kdoc_ref, q_ref, do_ref, k_ref, v_ref, out_ref, dq_ref, dk_ref, dv_ref):
    block = pl.program_id(0)
    head = pl.program_id(1)
    window_rows = BAND * BLOCK
    scale = HEAD_DIM ** (-0.5)

    @pl.when((block == 0) & (head == 0))
    def _():
        dk_ref[...] = jnp.zeros_like(dk_ref)
        dv_ref[...] = jnp.zeros_like(dv_ref)

    start = pl.multiple_of(block * BLOCK, BLOCK)
    key_window = k_ref[pl.ds(start, window_rows), :]
    value_window = v_ref[pl.ds(start, window_rows), :]
    query = q_ref[0]
    raw = lax.dot_general(query, key_window, TRANS_B, preferred_element_type=jnp.float32) * scale
    rows = lax.broadcasted_iota(jnp.int32, raw.shape, 0) + (BAND - 1) * BLOCK
    cols = lax.broadcasted_iota(jnp.int32, raw.shape, 1)
    allowed = (qdoc_ref[0] == kdoc_ref[0]) & (cols <= rows)
    scores = jnp.where(allowed, raw, -1e30)
    row_max = jnp.max(scores, axis=1, keepdims=True)
    log_total = row_max + jnp.log(jnp.sum(jnp.exp(scores - row_max), axis=1, keepdims=True))
    weights = jnp.exp(scores - log_total)
    soft_low = weights.astype(jnp.bfloat16)
    out = jnp.dot(soft_low, value_window, preferred_element_type=jnp.float32).astype(jnp.bfloat16)
    out_ref[0] = out
    grad = do_ref[0]
    row_dot = jnp.sum(grad.astype(jnp.float32) * out.astype(jnp.float32), axis=1, keepdims=True)
    prob_grad = lax.dot_general(grad, value_window, TRANS_B, preferred_element_type=jnp.float32)
    score_grad = (weights * (prob_grad - row_dot)).astype(jnp.bfloat16)
    dq = jnp.dot(score_grad, key_window, preferred_element_type=jnp.float32) * scale
    dq_ref[0] = dq.astype(jnp.bfloat16)
    dk = lax.dot_general(score_grad, query, TRANS_A, preferred_element_type=jnp.float32) * scale
    dv = lax.dot_general(soft_low, grad, TRANS_A, preferred_element_type=jnp.float32)
    dk_ref[pl.ds(start, window_rows), :] += dk
    dv_ref[pl.ds(start, window_rows), :] += dv


def fused_attention(query_blocks, grad_blocks, halo_key, halo_value, halo_doc):
    blocks, _, width = query_blocks.shape
    heads_here = width // HEAD_DIM
    window_rows = BAND * BLOCK
    reach = (BAND - 1) * BLOCK
    halo_rows = halo_key.shape[0]
    query_doc = halo_doc[reach:].reshape(blocks, BLOCK, 1)
    key_doc = jnp.stack(
        [halo_doc[b * BLOCK : b * BLOCK + window_rows] for b in range(blocks)]
    ).reshape(blocks, 1, window_rows)
    head_spec = pl.BlockSpec((1, BLOCK, HEAD_DIM), lambda b, h: (b, 0, h))
    whole = pl.BlockSpec((halo_rows, HEAD_DIM), lambda b, h: (0, 0))
    return pl.pallas_call(
        fused_kernel,
        grid=(blocks, heads_here),
        in_specs=[
            pl.BlockSpec((1, BLOCK, 1), lambda b, h: (b, 0, 0)),
            pl.BlockSpec((1, 1, window_rows), lambda b, h: (b, 0, 0)),
            head_spec,
            head_spec,
            whole,
            whole,
        ],
        out_specs=[head_spec, head_spec, whole, whole],
        out_shape=[
            jax.ShapeDtypeStruct(query_blocks.shape, jnp.bfloat16),
            jax.ShapeDtypeStruct(query_blocks.shape, jnp.bfloat16),
            jax.ShapeDtypeStruct((halo_rows, HEAD_DIM), jnp.float32),
            jax.ShapeDtypeStruct((halo_rows, HEAD_DIM), jnp.float32),
        ],
        compiler_params=pltpu.CompilerParams(dimension_semantics=("arbitrary", "arbitrary")),
    )(query_doc, key_doc, query_blocks, grad_blocks, halo_key, halo_value)


def shift_from_below(x, ctx_count, distance):
    pairs = [(s, s + distance) for s in range(ctx_count - distance)]
    return lax.ppermute(x, "ctx", pairs)


def shift_to_below(x, ctx_count, distance):
    pairs = [(s + distance, s) for s in range(ctx_count - distance)]
    return lax.ppermute(x, "ctx", pairs)


def on_device(queries, key_rows, value_rows, out_grad, doc_ids, block_owner):
    ctx_count = lax.axis_size("ctx")
    tp_count = lax.axis_size("tp")
    ctx_rank = lax.axis_index("ctx")
    local_rows, width = queries.shape
    head_cols = width // tp_count
    tok_dev = key_rows.shape[0]
    kv_cols = key_rows.shape[1]
    blocks_here = tok_dev // BLOCK
    reach = (BAND - 1) * BLOCK
    far = reach - tok_dev
    send_pick, recv_pick, _ = routing(block_owner, ctx_count, ctx_rank, blocks_here)
    query_split, grad_split = (
        lax.all_to_all(
            queries.reshape(local_rows, tp_count, head_cols),
            "tp",
            split_axis=1,
            concat_axis=0,
            tiled=True,
        ),
        lax.all_to_all(
            out_grad.reshape(local_rows, tp_count, head_cols),
            "tp",
            split_axis=1,
            concat_axis=0,
            tiled=True,
        ),
    )
    query_blocks = query_split.reshape(blocks_here, BLOCK, head_cols)
    grad_blocks = grad_split.reshape(blocks_here, BLOCK, head_cols)
    kv_here = jnp.concatenate([key_rows, value_rows], axis=1)
    kv_near = shift_from_below(kv_here, ctx_count, 1)
    kv_far = shift_from_below(kv_here[tok_dev - far :], ctx_count, 2)
    halo = jnp.concatenate([kv_far, kv_near, kv_here], axis=0)
    halo_key = halo[:, :kv_cols]
    halo_value = halo[:, kv_cols:]
    halo_doc = halo_docs(doc_ids, ctx_rank * tok_dev - reach, reach + tok_dev)
    out_blocks, dq_blocks, key_grad, value_grad = fused_attention(
        query_blocks, grad_blocks, halo_key, halo_value, halo_doc
    )
    kv_grad = jnp.concatenate([key_grad, value_grad], axis=1)
    grad_near = shift_to_below(kv_grad[far:reach], ctx_count, 1)
    grad_far = shift_to_below(kv_grad[:far], ctx_count, 2)
    kv_total = kv_grad[reach:] + grad_near
    kv_total = kv_total.at[tok_dev - far :].add(grad_far)
    sent_out, sent_dq = (
        lax.all_to_all(
            select_rows(send_pick, out_blocks), "ctx", split_axis=0, concat_axis=0, tiled=True
        ),
        lax.all_to_all(
            select_rows(send_pick, dq_blocks), "ctx", split_axis=0, concat_axis=0, tiled=True
        ),
    )
    held_out = select_rows(recv_pick, sent_out)
    held_dq = select_rows(recv_pick, sent_dq)
    return (
        held_out.reshape(tok_dev, head_cols),
        held_dq.reshape(tok_dev, head_cols),
        kv_total[:, :kv_cols].astype(jnp.bfloat16),
        kv_total[:, kv_cols:].astype(jnp.bfloat16),
    )


def solution(mesh):
    return jax.shard_map(
        on_device,
        mesh=mesh,
        in_specs=(
            P(("ctx", "tp"), None),
            P("ctx", "tp"),
            P("ctx", "tp"),
            P(("ctx", "tp"), None),
            P(),
            P(),
        ),
        out_specs=(P("ctx", "tp"), P("ctx", "tp"), P("ctx", "tp"), P("ctx", "tp")),
        check_vma=False,
    )
```

```python
import jax
import jax.numpy as jnp
from jax import lax
from jax.sharding import PartitionSpec as P
from jax.experimental import pallas as pl
from jax.experimental.pallas import tpu as pltpu

HEADS = 64
KV_HEADS = 8
HEAD_DIM = 128
BLOCK = 128
BAND = 12
CHUNKS = 2


def routing(block_owner, ctx_count, ctx_rank, blocks_here):
    owner_grid = block_owner.reshape(ctx_count, blocks_here)
    own_targets = lax.dynamic_index_in_dim(owner_grid, ctx_rank, 0, keepdims=False)
    targets = jnp.arange(ctx_count, dtype=jnp.int32)
    send_pick = (own_targets[None, :] == targets[:, None]).astype(jnp.bfloat16)
    arrivals = (owner_grid == ctx_rank).astype(jnp.int32)
    present = jnp.sum(arrivals, axis=1)
    arrival_rank = jnp.cumsum(present) - 1
    slot_index = jnp.arange(blocks_here, dtype=jnp.int32)
    chosen = (present[None, :] == 1) & (arrival_rank[None, :] == slot_index[:, None])
    source_block = targets * blocks_here + jnp.sum(arrivals * slot_index[None, :], axis=1)
    held_ids = jnp.sum(chosen.astype(jnp.int32) * source_block[None, :], axis=1)
    return (send_pick, chosen.astype(jnp.bfloat16), held_ids)


def select_rows(selector, blocks):
    picked = jnp.einsum("ab,brh->arh", selector, blocks, preferred_element_type=jnp.float32)
    return picked.astype(jnp.bfloat16)


def halo_docs(doc_ids, first_row, halo_rows):
    positions = first_row + jnp.arange(halo_rows, dtype=jnp.int32)
    picked = jnp.take(doc_ids, jnp.clip(positions, 0, doc_ids.shape[0] - 1), axis=0)
    return jnp.where(positions >= 0, picked, -1)


def masked_scores(query_block, key_window, query_doc, key_doc, local_block):
    window_rows = key_window.shape[0]
    kv_local = key_window.shape[1]
    query_heads = query_block.reshape(BLOCK, kv_local, HEADS // KV_HEADS, HEAD_DIM)
    raw_scores = jnp.einsum(
        "qkgd,wkd->kgqw", query_heads, key_window, preferred_element_type=jnp.float32
    ) * HEAD_DIM ** (-0.5)
    query_pos = (BAND - 1) * BLOCK + jnp.arange(BLOCK, dtype=jnp.int32)
    key_pos = jnp.arange(window_rows, dtype=jnp.int32)
    allowed = (query_doc[:, None] == key_doc[None, :]) & (key_pos[None, :] <= query_pos[:, None])
    return (jnp.where(allowed[None, None], raw_scores, -1e30), query_heads)


def window_of(halo_key, halo_value, halo_doc, local_block):
    window_rows = BAND * BLOCK
    kv_local = halo_key.shape[1] // HEAD_DIM
    start = local_block * BLOCK
    key_window = lax.dynamic_slice_in_dim(halo_key, start, window_rows, 0)
    value_window = lax.dynamic_slice_in_dim(halo_value, start, window_rows, 0)
    key_doc = lax.dynamic_slice_in_dim(halo_doc, start, window_rows, 0)
    query_doc = lax.dynamic_slice_in_dim(halo_doc, start + (BAND - 1) * BLOCK, BLOCK, 0)
    return (
        key_window.reshape(window_rows, kv_local, HEAD_DIM),
        value_window.reshape(window_rows, kv_local, HEAD_DIM),
        query_doc,
        key_doc,
    )


def attend_forward(query_blocks, halo_key, halo_value, halo_doc):

    def advance(running, inputs):
        query_block, local_block = inputs
        key_window, value_window, query_doc, key_doc = window_of(
            halo_key, halo_value, halo_doc, local_block
        )
        scores, _ = masked_scores(query_block, key_window, query_doc, key_doc, local_block)
        row_max = jnp.max(scores, axis=-1, keepdims=True)
        log_total = row_max + jnp.log(jnp.sum(jnp.exp(scores - row_max), axis=-1, keepdims=True))
        soft_low = jnp.exp(scores - log_total).astype(jnp.bfloat16)
        natural_out = jnp.einsum(
            "kgqw,wkd->qkgd", soft_low, value_window, preferred_element_type=jnp.float32
        )
        return (running, (natural_out.reshape(BLOCK, -1).astype(jnp.bfloat16), log_total))

    local_ids = jnp.arange(query_blocks.shape[0], dtype=jnp.int32)
    _, (out_blocks, log_totals) = lax.scan(
        advance, jnp.zeros((), jnp.float32), (query_blocks, local_ids)
    )
    return (out_blocks, log_totals)


def attend_backward(query_blocks, grad_blocks, out_blocks, log_totals, halo_key, halo_value, halo_doc):
    window_rows = BAND * BLOCK
    inv_root = HEAD_DIM ** (-0.5)

    def advance(running, inputs):
        key_grad, value_grad = running
        query_block, grad_block, out_block, log_total, local_block = inputs
        key_window, value_window, query_doc, key_doc = window_of(
            halo_key, halo_value, halo_doc, local_block
        )
        scores, query_heads = masked_scores(
            query_block, key_window, query_doc, key_doc, local_block
        )
        grad_heads = grad_block.reshape(query_heads.shape)
        out_heads = out_block.reshape(query_heads.shape)
        weights = jnp.exp(scores - log_total)
        soft_low = weights.astype(jnp.bfloat16)
        row_dot = jnp.sum(grad_heads.astype(jnp.float32) * out_heads.astype(jnp.float32), axis=-1)
        row_dot = jnp.transpose(row_dot, (1, 2, 0))[..., None]
        prob_grad = jnp.einsum(
            "qkgd,wkd->kgqw", grad_heads, value_window, preferred_element_type=jnp.float32
        )
        score_grad = (weights * (prob_grad - row_dot)).astype(jnp.bfloat16)
        query_part = (
            jnp.einsum("kgqw,wkd->qkgd", score_grad, key_window, preferred_element_type=jnp.float32)
            * inv_root
        )
        key_part = (
            jnp.einsum(
                "kgqw,qkgd->wkd", score_grad, query_heads, preferred_element_type=jnp.float32
            )
            * inv_root
        )
        value_part = jnp.einsum(
            "kgqw,qkgd->wkd", soft_low, grad_heads, preferred_element_type=jnp.float32
        )
        start = local_block * BLOCK
        old_keys = lax.dynamic_slice_in_dim(key_grad, start, window_rows, 0)
        old_values = lax.dynamic_slice_in_dim(value_grad, start, window_rows, 0)
        key_grad = lax.dynamic_update_slice_in_dim(
            key_grad, old_keys + key_part.reshape(window_rows, -1), start, 0
        )
        value_grad = lax.dynamic_update_slice_in_dim(
            value_grad, old_values + value_part.reshape(window_rows, -1), start, 0
        )
        return ((key_grad, value_grad), query_part.reshape(BLOCK, -1).astype(jnp.bfloat16))

    zero_grads = (
        jnp.zeros(halo_key.shape, jnp.float32),
        jnp.zeros(halo_value.shape, jnp.float32),
    )
    local_ids = jnp.arange(query_blocks.shape[0], dtype=jnp.int32)
    (key_grad, value_grad), dq_blocks = lax.scan(
        advance, zero_grads, (query_blocks, grad_blocks, out_blocks, log_totals, local_ids)
    )
    return (dq_blocks, key_grad, value_grad)


TRANS_B = (((1,), (1,)), ((), ()))
TRANS_A = (((0,), (0,)), ((), ()))


def fused_kernel(qdoc_ref, kdoc_ref, q_ref, do_ref, k_ref, v_ref, out_ref, dq_ref, dk_ref, dv_ref):
    block = pl.program_id(0)
    head = pl.program_id(1)
    window_rows = BAND * BLOCK
    scale = HEAD_DIM ** (-0.5)

    @pl.when((block == 0) & (head == 0))
    def _():
        dk_ref[...] = jnp.zeros_like(dk_ref)
        dv_ref[...] = jnp.zeros_like(dv_ref)

    start = pl.multiple_of(block * BLOCK, BLOCK)
    key_window = k_ref[pl.ds(start, window_rows), :]
    value_window = v_ref[pl.ds(start, window_rows), :]
    query = q_ref[0]
    raw = lax.dot_general(query, key_window, TRANS_B, preferred_element_type=jnp.float32) * scale
    rows = lax.broadcasted_iota(jnp.int32, raw.shape, 0) + (BAND - 1) * BLOCK
    cols = lax.broadcasted_iota(jnp.int32, raw.shape, 1)
    allowed = (qdoc_ref[0] == kdoc_ref[0]) & (cols <= rows)
    scores = jnp.where(allowed, raw, -1e30)
    row_max = jnp.max(scores, axis=1, keepdims=True)
    log_total = row_max + jnp.log(jnp.sum(jnp.exp(scores - row_max), axis=1, keepdims=True))
    weights = jnp.exp(scores - log_total)
    soft_low = weights.astype(jnp.bfloat16)
    out = jnp.dot(soft_low, value_window, preferred_element_type=jnp.float32).astype(jnp.bfloat16)
    out_ref[0] = out
    grad = do_ref[0]
    row_dot = jnp.sum(grad.astype(jnp.float32) * out.astype(jnp.float32), axis=1, keepdims=True)
    prob_grad = lax.dot_general(grad, value_window, TRANS_B, preferred_element_type=jnp.float32)
    score_grad = (weights * (prob_grad - row_dot)).astype(jnp.bfloat16)
    dq = jnp.dot(score_grad, key_window, preferred_element_type=jnp.float32) * scale
    dq_ref[0] = dq.astype(jnp.bfloat16)
    dk = lax.dot_general(score_grad, query, TRANS_A, preferred_element_type=jnp.float32) * scale
    dv = lax.dot_general(soft_low, grad, TRANS_A, preferred_element_type=jnp.float32)
    dk_ref[pl.ds(start, window_rows), :] += dk
    dv_ref[pl.ds(start, window_rows), :] += dv


def fused_attention(query_blocks, grad_blocks, halo_key, halo_value, halo_doc):
    blocks, _, width = query_blocks.shape
    heads_here = width // HEAD_DIM
    window_rows = BAND * BLOCK
    reach = (BAND - 1) * BLOCK
    halo_rows = halo_key.shape[0]
    query_doc = halo_doc[reach:].reshape(blocks, BLOCK, 1)
    key_doc = jnp.stack(
        [halo_doc[b * BLOCK : b * BLOCK + window_rows] for b in range(blocks)]
    ).reshape(blocks, 1, window_rows)
    head_spec = pl.BlockSpec((1, BLOCK, HEAD_DIM), lambda b, h: (b, 0, h))
    whole = pl.BlockSpec((halo_rows, HEAD_DIM), lambda b, h: (0, 0))
    return pl.pallas_call(
        fused_kernel,
        grid=(blocks, heads_here),
        in_specs=[
            pl.BlockSpec((1, BLOCK, 1), lambda b, h: (b, 0, 0)),
            pl.BlockSpec((1, 1, window_rows), lambda b, h: (b, 0, 0)),
            head_spec,
            head_spec,
            whole,
            whole,
        ],
        out_specs=[head_spec, head_spec, whole, whole],
        out_shape=[
            jax.ShapeDtypeStruct(query_blocks.shape, jnp.bfloat16),
            jax.ShapeDtypeStruct(query_blocks.shape, jnp.bfloat16),
            jax.ShapeDtypeStruct((halo_rows, HEAD_DIM), jnp.float32),
            jax.ShapeDtypeStruct((halo_rows, HEAD_DIM), jnp.float32),
        ],
        compiler_params=pltpu.CompilerParams(dimension_semantics=("arbitrary", "arbitrary")),
    )(query_doc, key_doc, query_blocks, grad_blocks, halo_key, halo_value)


def shift_from_below(x, ctx_count, distance):
    pairs = [(s, s + distance) for s in range(ctx_count - distance)]
    return lax.ppermute(x, "ctx", pairs)


def shift_to_below(x, ctx_count, distance):
    pairs = [(s + distance, s) for s in range(ctx_count - distance)]
    return lax.ppermute(x, "ctx", pairs)


def on_device(queries, key_rows, value_rows, out_grad, doc_ids, block_owner):
    ctx_count = lax.axis_size("ctx")
    tp_count = lax.axis_size("tp")
    ctx_rank = lax.axis_index("ctx")
    local_rows, width = queries.shape
    head_cols = width // tp_count
    chunk_cols = head_cols // CHUNKS
    tok_dev = key_rows.shape[0]
    kv_cols = key_rows.shape[1]
    blocks_here = tok_dev // BLOCK
    reach = (BAND - 1) * BLOCK
    far = reach - tok_dev
    send_pick, recv_pick, _ = routing(block_owner, ctx_count, ctx_rank, blocks_here)
    kv_here = jnp.concatenate([key_rows, value_rows], axis=1)
    kv_near = shift_from_below(kv_here, ctx_count, 1)
    kv_far = shift_from_below(kv_here[tok_dev - far :], ctx_count, 2)
    halo = jnp.concatenate([kv_far, kv_near, kv_here], axis=0)
    halo_key = halo[:, :kv_cols]
    halo_value = halo[:, kv_cols:]
    padded_doc = jnp.concatenate([jnp.full((reach,), -1, doc_ids.dtype), doc_ids])
    halo_doc = lax.dynamic_slice_in_dim(padded_doc, ctx_rank * tok_dev, reach + tok_dev, 0)
    query_parts = queries.reshape(local_rows, tp_count, CHUNKS, chunk_cols)
    grad_parts = out_grad.reshape(local_rows, tp_count, CHUNKS, chunk_cols)
    held_parts = []
    key_grad = None
    for chunk in range(CHUNKS):
        both = jnp.concatenate([query_parts[:, :, chunk], grad_parts[:, :, chunk]], axis=-1)
        both = lax.all_to_all(both, "tp", split_axis=1, concat_axis=0, tiled=True)
        both = both.reshape(blocks_here, BLOCK, 2 * chunk_cols)
        out_blocks, dq_blocks, chunk_key_grad, chunk_value_grad = fused_attention(
            both[..., :chunk_cols], both[..., chunk_cols:], halo_key, halo_value, halo_doc
        )
        if key_grad is None:
            key_grad, value_grad = chunk_key_grad, chunk_value_grad
        else:
            key_grad = key_grad + chunk_key_grad
            value_grad = value_grad + chunk_value_grad
        results = jnp.concatenate([out_blocks, dq_blocks], axis=-1)
        sent = lax.all_to_all(
            select_rows(send_pick, results), "ctx", split_axis=0, concat_axis=0, tiled=True
        )
        held_parts.append(select_rows(recv_pick, sent))
    kv_grad = jnp.concatenate([key_grad, value_grad], axis=1)
    grad_near = shift_to_below(kv_grad[far:reach], ctx_count, 1)
    grad_far = shift_to_below(kv_grad[:far], ctx_count, 2)
    kv_total = kv_grad[reach:] + grad_near
    kv_total = kv_total.at[tok_dev - far :].add(grad_far)
    held_out = jnp.concatenate([part[..., :chunk_cols] for part in held_parts], axis=-1)
    held_dq = jnp.concatenate([part[..., chunk_cols:] for part in held_parts], axis=-1)
    return (
        held_out.reshape(tok_dev, head_cols),
        held_dq.reshape(tok_dev, head_cols),
        kv_total[:, :kv_cols].astype(jnp.bfloat16),
        kv_total[:, kv_cols:].astype(jnp.bfloat16),
    )


def solution(mesh):
    return jax.shard_map(
        on_device,
        mesh=mesh,
        in_specs=(
            P(("ctx", "tp"), None),
            P("ctx", "tp"),
            P("ctx", "tp"),
            P(("ctx", "tp"), None),
            P(),
            P(),
        ),
        out_specs=(P("ctx", "tp"), P("ctx", "tp"), P("ctx", "tp"), P("ctx", "tp")),
        check_vma=False,
    )
```

```python
import jax
import jax.numpy as jnp
from jax import lax
from jax.sharding import PartitionSpec as P
from jax.experimental import pallas as pl
from jax.experimental.pallas import tpu as pltpu

HEADS = 64
KV_HEADS = 8
HEAD_DIM = 128
BLOCK = 128
BAND = 12
CHUNKS = 2


def routing(block_owner, ctx_count, ctx_rank, blocks_here):
    owner_grid = block_owner.reshape(ctx_count, blocks_here)
    own_targets = lax.dynamic_index_in_dim(owner_grid, ctx_rank, 0, keepdims=False)
    targets = jnp.arange(ctx_count, dtype=jnp.int32)
    send_pick = (own_targets[None, :] == targets[:, None]).astype(jnp.bfloat16)
    arrivals = (owner_grid == ctx_rank).astype(jnp.int32)
    present = jnp.sum(arrivals, axis=1)
    arrival_rank = jnp.cumsum(present) - 1
    slot_index = jnp.arange(blocks_here, dtype=jnp.int32)
    chosen = (present[None, :] == 1) & (arrival_rank[None, :] == slot_index[:, None])
    source_block = targets * blocks_here + jnp.sum(arrivals * slot_index[None, :], axis=1)
    held_ids = jnp.sum(chosen.astype(jnp.int32) * source_block[None, :], axis=1)
    return (send_pick, chosen.astype(jnp.bfloat16), held_ids)


def select_rows(selector, blocks):
    picked = jnp.einsum("ab,brh->arh", selector, blocks, preferred_element_type=jnp.float32)
    return picked.astype(jnp.bfloat16)


def halo_docs(doc_ids, first_row, halo_rows):
    positions = first_row + jnp.arange(halo_rows, dtype=jnp.int32)
    picked = jnp.take(doc_ids, jnp.clip(positions, 0, doc_ids.shape[0] - 1), axis=0)
    return jnp.where(positions >= 0, picked, -1)


def masked_scores(query_block, key_window, query_doc, key_doc, local_block):
    window_rows = key_window.shape[0]
    kv_local = key_window.shape[1]
    query_heads = query_block.reshape(BLOCK, kv_local, HEADS // KV_HEADS, HEAD_DIM)
    raw_scores = jnp.einsum(
        "qkgd,wkd->kgqw", query_heads, key_window, preferred_element_type=jnp.float32
    ) * HEAD_DIM ** (-0.5)
    query_pos = (BAND - 1) * BLOCK + jnp.arange(BLOCK, dtype=jnp.int32)
    key_pos = jnp.arange(window_rows, dtype=jnp.int32)
    allowed = (query_doc[:, None] == key_doc[None, :]) & (key_pos[None, :] <= query_pos[:, None])
    return (jnp.where(allowed[None, None], raw_scores, -1e30), query_heads)


def window_of(halo_key, halo_value, halo_doc, local_block):
    window_rows = BAND * BLOCK
    kv_local = halo_key.shape[1] // HEAD_DIM
    start = local_block * BLOCK
    key_window = lax.dynamic_slice_in_dim(halo_key, start, window_rows, 0)
    value_window = lax.dynamic_slice_in_dim(halo_value, start, window_rows, 0)
    key_doc = lax.dynamic_slice_in_dim(halo_doc, start, window_rows, 0)
    query_doc = lax.dynamic_slice_in_dim(halo_doc, start + (BAND - 1) * BLOCK, BLOCK, 0)
    return (
        key_window.reshape(window_rows, kv_local, HEAD_DIM),
        value_window.reshape(window_rows, kv_local, HEAD_DIM),
        query_doc,
        key_doc,
    )


def attend_forward(query_blocks, halo_key, halo_value, halo_doc):

    def advance(running, inputs):
        query_block, local_block = inputs
        key_window, value_window, query_doc, key_doc = window_of(
            halo_key, halo_value, halo_doc, local_block
        )
        scores, _ = masked_scores(query_block, key_window, query_doc, key_doc, local_block)
        row_max = jnp.max(scores, axis=-1, keepdims=True)
        log_total = row_max + jnp.log(jnp.sum(jnp.exp(scores - row_max), axis=-1, keepdims=True))
        soft_low = jnp.exp(scores - log_total).astype(jnp.bfloat16)
        natural_out = jnp.einsum(
            "kgqw,wkd->qkgd", soft_low, value_window, preferred_element_type=jnp.float32
        )
        return (running, (natural_out.reshape(BLOCK, -1).astype(jnp.bfloat16), log_total))

    local_ids = jnp.arange(query_blocks.shape[0], dtype=jnp.int32)
    _, (out_blocks, log_totals) = lax.scan(
        advance, jnp.zeros((), jnp.float32), (query_blocks, local_ids)
    )
    return (out_blocks, log_totals)


def attend_backward(query_blocks, grad_blocks, out_blocks, log_totals, halo_key, halo_value, halo_doc):
    window_rows = BAND * BLOCK
    inv_root = HEAD_DIM ** (-0.5)

    def advance(running, inputs):
        key_grad, value_grad = running
        query_block, grad_block, out_block, log_total, local_block = inputs
        key_window, value_window, query_doc, key_doc = window_of(
            halo_key, halo_value, halo_doc, local_block
        )
        scores, query_heads = masked_scores(
            query_block, key_window, query_doc, key_doc, local_block
        )
        grad_heads = grad_block.reshape(query_heads.shape)
        out_heads = out_block.reshape(query_heads.shape)
        weights = jnp.exp(scores - log_total)
        soft_low = weights.astype(jnp.bfloat16)
        row_dot = jnp.sum(grad_heads.astype(jnp.float32) * out_heads.astype(jnp.float32), axis=-1)
        row_dot = jnp.transpose(row_dot, (1, 2, 0))[..., None]
        prob_grad = jnp.einsum(
            "qkgd,wkd->kgqw", grad_heads, value_window, preferred_element_type=jnp.float32
        )
        score_grad = (weights * (prob_grad - row_dot)).astype(jnp.bfloat16)
        query_part = (
            jnp.einsum("kgqw,wkd->qkgd", score_grad, key_window, preferred_element_type=jnp.float32)
            * inv_root
        )
        key_part = (
            jnp.einsum(
                "kgqw,qkgd->wkd", score_grad, query_heads, preferred_element_type=jnp.float32
            )
            * inv_root
        )
        value_part = jnp.einsum(
            "kgqw,qkgd->wkd", soft_low, grad_heads, preferred_element_type=jnp.float32
        )
        start = local_block * BLOCK
        old_keys = lax.dynamic_slice_in_dim(key_grad, start, window_rows, 0)
        old_values = lax.dynamic_slice_in_dim(value_grad, start, window_rows, 0)
        key_grad = lax.dynamic_update_slice_in_dim(
            key_grad, old_keys + key_part.reshape(window_rows, -1), start, 0
        )
        value_grad = lax.dynamic_update_slice_in_dim(
            value_grad, old_values + value_part.reshape(window_rows, -1), start, 0
        )
        return ((key_grad, value_grad), query_part.reshape(BLOCK, -1).astype(jnp.bfloat16))

    zero_grads = (
        jnp.zeros(halo_key.shape, jnp.float32),
        jnp.zeros(halo_value.shape, jnp.float32),
    )
    local_ids = jnp.arange(query_blocks.shape[0], dtype=jnp.int32)
    (key_grad, value_grad), dq_blocks = lax.scan(
        advance, zero_grads, (query_blocks, grad_blocks, out_blocks, log_totals, local_ids)
    )
    return (dq_blocks, key_grad, value_grad)


TRANS_B = (((1,), (1,)), ((), ()))
TRANS_A = (((0,), (0,)), ((), ()))


def fused_kernel(qdoc_ref, kdoc_ref, q_ref, do_ref, k_ref, v_ref, out_ref, dq_ref, dk_ref, dv_ref):
    block = pl.program_id(0)
    window_rows = BAND * BLOCK
    scale = HEAD_DIM ** (-0.5)
    heads_here = q_ref.shape[2] // HEAD_DIM

    @pl.when(block == 0)
    def _():
        dk_ref[...] = jnp.zeros_like(dk_ref)
        dv_ref[...] = jnp.zeros_like(dv_ref)

    start = pl.multiple_of(block * BLOCK, BLOCK)
    key_window = k_ref[pl.ds(start, window_rows), :]
    value_window = v_ref[pl.ds(start, window_rows), :]
    shape = (BLOCK, window_rows)
    rows = lax.broadcasted_iota(jnp.int32, shape, 0) + (BAND - 1) * BLOCK
    cols = lax.broadcasted_iota(jnp.int32, shape, 1)
    allowed = (qdoc_ref[0] == kdoc_ref[0]) & (cols <= rows)
    bias = jnp.where(allowed, 0.0, -1e30).astype(jnp.float32)
    dk_sum = None
    for head in range(heads_here):
        cols_of = slice(head * HEAD_DIM, (head + 1) * HEAD_DIM)
        query = q_ref[0, :, cols_of]
        raw = lax.dot_general(query, key_window, TRANS_B, preferred_element_type=jnp.float32) * scale
        scores = raw + bias
        row_max = jnp.max(scores, axis=1, keepdims=True)
        log_total = row_max + jnp.log(jnp.sum(jnp.exp(scores - row_max), axis=1, keepdims=True))
        weights = jnp.exp(scores - log_total)
        soft_low = weights.astype(jnp.bfloat16)
        out = jnp.dot(soft_low, value_window, preferred_element_type=jnp.float32).astype(jnp.bfloat16)
        out_ref[0, :, cols_of] = out
        grad = do_ref[0, :, cols_of]
        row_dot = jnp.sum(grad.astype(jnp.float32) * out.astype(jnp.float32), axis=1, keepdims=True)
        prob_grad = lax.dot_general(grad, value_window, TRANS_B, preferred_element_type=jnp.float32)
        score_grad = (weights * (prob_grad - row_dot)).astype(jnp.bfloat16)
        dq = jnp.dot(score_grad, key_window, preferred_element_type=jnp.float32) * scale
        dq_ref[0, :, cols_of] = dq.astype(jnp.bfloat16)
        dk = lax.dot_general(score_grad, query, TRANS_A, preferred_element_type=jnp.float32) * scale
        dv = lax.dot_general(soft_low, grad, TRANS_A, preferred_element_type=jnp.float32)
        if dk_sum is None:
            dk_sum, dv_sum = dk, dv
        else:
            dk_sum, dv_sum = dk_sum + dk, dv_sum + dv
    dk_ref[pl.ds(start, window_rows), :] += dk_sum
    dv_ref[pl.ds(start, window_rows), :] += dv_sum


def fused_attention(query_blocks, grad_blocks, halo_key, halo_value, halo_doc):
    blocks, _, width = query_blocks.shape
    window_rows = BAND * BLOCK
    reach = (BAND - 1) * BLOCK
    halo_rows = halo_key.shape[0]
    query_doc = halo_doc[reach:].reshape(blocks, BLOCK, 1)
    key_doc = jnp.stack(
        [halo_doc[b * BLOCK : b * BLOCK + window_rows] for b in range(blocks)]
    ).reshape(blocks, 1, window_rows)
    block_spec = pl.BlockSpec((1, BLOCK, width), lambda b: (b, 0, 0))
    whole = pl.BlockSpec((halo_rows, HEAD_DIM), lambda b: (0, 0))
    return pl.pallas_call(
        fused_kernel,
        grid=(blocks,),
        in_specs=[
            pl.BlockSpec((1, BLOCK, 1), lambda b: (b, 0, 0)),
            pl.BlockSpec((1, 1, window_rows), lambda b: (b, 0, 0)),
            block_spec,
            block_spec,
            whole,
            whole,
        ],
        out_specs=[block_spec, block_spec, whole, whole],
        out_shape=[
            jax.ShapeDtypeStruct(query_blocks.shape, jnp.bfloat16),
            jax.ShapeDtypeStruct(query_blocks.shape, jnp.bfloat16),
            jax.ShapeDtypeStruct((halo_rows, HEAD_DIM), jnp.float32),
            jax.ShapeDtypeStruct((halo_rows, HEAD_DIM), jnp.float32),
        ],
        compiler_params=pltpu.CompilerParams(dimension_semantics=("arbitrary",)),
    )(query_doc, key_doc, query_blocks, grad_blocks, halo_key, halo_value)


def shift_from_below(x, ctx_count, distance):
    pairs = [(s, s + distance) for s in range(ctx_count - distance)]
    return lax.ppermute(x, "ctx", pairs)


def shift_to_below(x, ctx_count, distance):
    pairs = [(s + distance, s) for s in range(ctx_count - distance)]
    return lax.ppermute(x, "ctx", pairs)


def on_device(queries, key_rows, value_rows, out_grad, doc_ids, block_owner):
    ctx_count = lax.axis_size("ctx")
    tp_count = lax.axis_size("tp")
    ctx_rank = lax.axis_index("ctx")
    local_rows, width = queries.shape
    head_cols = width // tp_count
    chunk_cols = head_cols // CHUNKS
    tok_dev = key_rows.shape[0]
    kv_cols = key_rows.shape[1]
    blocks_here = tok_dev // BLOCK
    reach = (BAND - 1) * BLOCK
    far = reach - tok_dev
    send_pick, recv_pick, _ = routing(block_owner, ctx_count, ctx_rank, blocks_here)
    kv_here = jnp.concatenate([key_rows, value_rows], axis=1)
    kv_near = shift_from_below(kv_here, ctx_count, 1)
    kv_far = shift_from_below(kv_here[tok_dev - far :], ctx_count, 2)
    halo = jnp.concatenate([kv_far, kv_near, kv_here], axis=0)
    halo_key = halo[:, :kv_cols]
    halo_value = halo[:, kv_cols:]
    padded_doc = jnp.concatenate([jnp.full((reach,), -1, doc_ids.dtype), doc_ids])
    halo_doc = lax.dynamic_slice_in_dim(padded_doc, ctx_rank * tok_dev, reach + tok_dev, 0)
    query_parts = queries.reshape(local_rows, tp_count, CHUNKS, chunk_cols)
    grad_parts = out_grad.reshape(local_rows, tp_count, CHUNKS, chunk_cols)
    held_parts = []
    key_grad = None
    for chunk in range(CHUNKS):
        both = jnp.concatenate([query_parts[:, :, chunk], grad_parts[:, :, chunk]], axis=-1)
        both = lax.all_to_all(both, "tp", split_axis=1, concat_axis=0, tiled=True)
        both = both.reshape(blocks_here, BLOCK, 2 * chunk_cols)
        out_blocks, dq_blocks, chunk_key_grad, chunk_value_grad = fused_attention(
            both[..., :chunk_cols], both[..., chunk_cols:], halo_key, halo_value, halo_doc
        )
        if key_grad is None:
            key_grad, value_grad = chunk_key_grad, chunk_value_grad
        else:
            key_grad = key_grad + chunk_key_grad
            value_grad = value_grad + chunk_value_grad
        results = jnp.concatenate([out_blocks, dq_blocks], axis=-1)
        sent = lax.all_to_all(
            select_rows(send_pick, results), "ctx", split_axis=0, concat_axis=0, tiled=True
        )
        held_parts.append(select_rows(recv_pick, sent))
    kv_grad = jnp.concatenate([key_grad, value_grad], axis=1)
    grad_near = shift_to_below(kv_grad[far:reach], ctx_count, 1)
    grad_far = shift_to_below(kv_grad[:far], ctx_count, 2)
    kv_total = kv_grad[reach:] + grad_near
    kv_total = kv_total.at[tok_dev - far :].add(grad_far)
    held_out = jnp.concatenate([part[..., :chunk_cols] for part in held_parts], axis=-1)
    held_dq = jnp.concatenate([part[..., chunk_cols:] for part in held_parts], axis=-1)
    return (
        held_out.reshape(tok_dev, head_cols),
        held_dq.reshape(tok_dev, head_cols),
        kv_total[:, :kv_cols].astype(jnp.bfloat16),
        kv_total[:, kv_cols:].astype(jnp.bfloat16),
    )


def solution(mesh):
    return jax.shard_map(
        on_device,
        mesh=mesh,
        in_specs=(
            P(("ctx", "tp"), None),
            P("ctx", "tp"),
            P("ctx", "tp"),
            P(("ctx", "tp"), None),
            P(),
            P(),
        ),
        out_specs=(P("ctx", "tp"), P("ctx", "tp"), P("ctx", "tp"), P("ctx", "tp")),
        check_vma=False,
    )
```

```python
import jax
import jax.numpy as jnp
from jax import lax
from jax.sharding import PartitionSpec as P
from jax.experimental import pallas as pl
from jax.experimental.pallas import tpu as pltpu

HEADS = 64
KV_HEADS = 8
HEAD_DIM = 128
BLOCK = 128
BAND = 12
CHUNKS = 2


def routing(block_owner, ctx_count, ctx_rank, blocks_here):
    owner_grid = block_owner.reshape(ctx_count, blocks_here)
    own_targets = lax.dynamic_index_in_dim(owner_grid, ctx_rank, 0, keepdims=False)
    sources = jnp.arange(ctx_count, dtype=jnp.int32)
    present = jnp.sum((owner_grid == ctx_rank).astype(jnp.int32), axis=1)
    arrival_rank = jnp.cumsum(present) - 1
    slot_index = jnp.arange(blocks_here, dtype=jnp.int32)
    chosen = (present[None, :] == 1) & (arrival_rank[None, :] == slot_index[:, None])
    held_sources = jnp.sum(chosen.astype(jnp.int32) * sources[None, :], axis=1)
    return (own_targets, held_sources)


def select_rows(selector, blocks):
    picked = jnp.einsum("ab,brh->arh", selector, blocks, preferred_element_type=jnp.float32)
    return picked.astype(jnp.bfloat16)


def halo_docs(doc_ids, first_row, halo_rows):
    positions = first_row + jnp.arange(halo_rows, dtype=jnp.int32)
    picked = jnp.take(doc_ids, jnp.clip(positions, 0, doc_ids.shape[0] - 1), axis=0)
    return jnp.where(positions >= 0, picked, -1)


def masked_scores(query_block, key_window, query_doc, key_doc, local_block):
    window_rows = key_window.shape[0]
    kv_local = key_window.shape[1]
    query_heads = query_block.reshape(BLOCK, kv_local, HEADS // KV_HEADS, HEAD_DIM)
    raw_scores = jnp.einsum(
        "qkgd,wkd->kgqw", query_heads, key_window, preferred_element_type=jnp.float32
    ) * HEAD_DIM ** (-0.5)
    query_pos = (BAND - 1) * BLOCK + jnp.arange(BLOCK, dtype=jnp.int32)
    key_pos = jnp.arange(window_rows, dtype=jnp.int32)
    allowed = (query_doc[:, None] == key_doc[None, :]) & (key_pos[None, :] <= query_pos[:, None])
    return (jnp.where(allowed[None, None], raw_scores, -1e30), query_heads)


def window_of(halo_key, halo_value, halo_doc, local_block):
    window_rows = BAND * BLOCK
    kv_local = halo_key.shape[1] // HEAD_DIM
    start = local_block * BLOCK
    key_window = lax.dynamic_slice_in_dim(halo_key, start, window_rows, 0)
    value_window = lax.dynamic_slice_in_dim(halo_value, start, window_rows, 0)
    key_doc = lax.dynamic_slice_in_dim(halo_doc, start, window_rows, 0)
    query_doc = lax.dynamic_slice_in_dim(halo_doc, start + (BAND - 1) * BLOCK, BLOCK, 0)
    return (
        key_window.reshape(window_rows, kv_local, HEAD_DIM),
        value_window.reshape(window_rows, kv_local, HEAD_DIM),
        query_doc,
        key_doc,
    )


def attend_forward(query_blocks, halo_key, halo_value, halo_doc):

    def advance(running, inputs):
        query_block, local_block = inputs
        key_window, value_window, query_doc, key_doc = window_of(
            halo_key, halo_value, halo_doc, local_block
        )
        scores, _ = masked_scores(query_block, key_window, query_doc, key_doc, local_block)
        row_max = jnp.max(scores, axis=-1, keepdims=True)
        log_total = row_max + jnp.log(jnp.sum(jnp.exp(scores - row_max), axis=-1, keepdims=True))
        soft_low = jnp.exp(scores - log_total).astype(jnp.bfloat16)
        natural_out = jnp.einsum(
            "kgqw,wkd->qkgd", soft_low, value_window, preferred_element_type=jnp.float32
        )
        return (running, (natural_out.reshape(BLOCK, -1).astype(jnp.bfloat16), log_total))

    local_ids = jnp.arange(query_blocks.shape[0], dtype=jnp.int32)
    _, (out_blocks, log_totals) = lax.scan(
        advance, jnp.zeros((), jnp.float32), (query_blocks, local_ids)
    )
    return (out_blocks, log_totals)


def attend_backward(query_blocks, grad_blocks, out_blocks, log_totals, halo_key, halo_value, halo_doc):
    window_rows = BAND * BLOCK
    inv_root = HEAD_DIM ** (-0.5)

    def advance(running, inputs):
        key_grad, value_grad = running
        query_block, grad_block, out_block, log_total, local_block = inputs
        key_window, value_window, query_doc, key_doc = window_of(
            halo_key, halo_value, halo_doc, local_block
        )
        scores, query_heads = masked_scores(
            query_block, key_window, query_doc, key_doc, local_block
        )
        grad_heads = grad_block.reshape(query_heads.shape)
        out_heads = out_block.reshape(query_heads.shape)
        weights = jnp.exp(scores - log_total)
        soft_low = weights.astype(jnp.bfloat16)
        row_dot = jnp.sum(grad_heads.astype(jnp.float32) * out_heads.astype(jnp.float32), axis=-1)
        row_dot = jnp.transpose(row_dot, (1, 2, 0))[..., None]
        prob_grad = jnp.einsum(
            "qkgd,wkd->kgqw", grad_heads, value_window, preferred_element_type=jnp.float32
        )
        score_grad = (weights * (prob_grad - row_dot)).astype(jnp.bfloat16)
        query_part = (
            jnp.einsum("kgqw,wkd->qkgd", score_grad, key_window, preferred_element_type=jnp.float32)
            * inv_root
        )
        key_part = (
            jnp.einsum(
                "kgqw,qkgd->wkd", score_grad, query_heads, preferred_element_type=jnp.float32
            )
            * inv_root
        )
        value_part = jnp.einsum(
            "kgqw,qkgd->wkd", soft_low, grad_heads, preferred_element_type=jnp.float32
        )
        start = local_block * BLOCK
        old_keys = lax.dynamic_slice_in_dim(key_grad, start, window_rows, 0)
        old_values = lax.dynamic_slice_in_dim(value_grad, start, window_rows, 0)
        key_grad = lax.dynamic_update_slice_in_dim(
            key_grad, old_keys + key_part.reshape(window_rows, -1), start, 0
        )
        value_grad = lax.dynamic_update_slice_in_dim(
            value_grad, old_values + value_part.reshape(window_rows, -1), start, 0
        )
        return ((key_grad, value_grad), query_part.reshape(BLOCK, -1).astype(jnp.bfloat16))

    zero_grads = (
        jnp.zeros(halo_key.shape, jnp.float32),
        jnp.zeros(halo_value.shape, jnp.float32),
    )
    local_ids = jnp.arange(query_blocks.shape[0], dtype=jnp.int32)
    (key_grad, value_grad), dq_blocks = lax.scan(
        advance, zero_grads, (query_blocks, grad_blocks, out_blocks, log_totals, local_ids)
    )
    return (dq_blocks, key_grad, value_grad)


TRANS_B = (((1,), (1,)), ((), ()))
TRANS_A = (((0,), (0,)), ((), ()))


def fused_kernel(slot_ref, qdoc_ref, kdoc_ref, q_ref, do_ref, k_ref, v_ref, res_ref, dk_ref, dv_ref):
    block = pl.program_id(0)
    window_rows = BAND * BLOCK
    scale = HEAD_DIM ** (-0.5)
    width = q_ref.shape[2]
    heads_here = width // HEAD_DIM

    @pl.when(block == 0)
    def _():
        dk_ref[...] = jnp.zeros_like(dk_ref)
        dv_ref[...] = jnp.zeros_like(dv_ref)

    start = pl.multiple_of(block * BLOCK, BLOCK)
    key_window = k_ref[pl.ds(start, window_rows), :]
    value_window = v_ref[pl.ds(start, window_rows), :]
    shape = (BLOCK, window_rows)
    rows = lax.broadcasted_iota(jnp.int32, shape, 0) + (BAND - 1) * BLOCK
    cols = lax.broadcasted_iota(jnp.int32, shape, 1)
    allowed = (qdoc_ref[0] == kdoc_ref[0]) & (cols <= rows)
    bias = jnp.where(allowed, 0.0, -1e30).astype(jnp.float32)
    dk_sum = None
    for head in range(heads_here):
        cols_of = slice(head * HEAD_DIM, (head + 1) * HEAD_DIM)
        query = q_ref[0, :, cols_of]
        raw = lax.dot_general(query, key_window, TRANS_B, preferred_element_type=jnp.float32) * scale
        scores = raw + bias
        row_max = jnp.max(scores, axis=1, keepdims=True)
        log_total = row_max + jnp.log(jnp.sum(jnp.exp(scores - row_max), axis=1, keepdims=True))
        weights = jnp.exp(scores - log_total)
        soft_low = weights.astype(jnp.bfloat16)
        out = jnp.dot(soft_low, value_window, preferred_element_type=jnp.float32).astype(jnp.bfloat16)
        res_ref[0, :, cols_of] = out
        grad = do_ref[0, :, cols_of]
        row_dot = jnp.sum(grad.astype(jnp.float32) * out.astype(jnp.float32), axis=1, keepdims=True)
        prob_grad = lax.dot_general(grad, value_window, TRANS_B, preferred_element_type=jnp.float32)
        score_grad = (weights * (prob_grad - row_dot)).astype(jnp.bfloat16)
        dq = jnp.dot(score_grad, key_window, preferred_element_type=jnp.float32) * scale
        res_ref[0, :, width + head * HEAD_DIM : width + (head + 1) * HEAD_DIM] = dq.astype(
            jnp.bfloat16
        )
        dk = lax.dot_general(score_grad, query, TRANS_A, preferred_element_type=jnp.float32) * scale
        dv = lax.dot_general(soft_low, grad, TRANS_A, preferred_element_type=jnp.float32)
        if dk_sum is None:
            dk_sum, dv_sum = dk, dv
        else:
            dk_sum, dv_sum = dk_sum + dk, dv_sum + dv
    dk_ref[pl.ds(start, window_rows), :] += dk_sum
    dv_ref[pl.ds(start, window_rows), :] += dv_sum


def fused_attention(slots, query_blocks, grad_blocks, halo_key, halo_value, halo_doc, slot_count):
    blocks, _, width = query_blocks.shape
    window_rows = BAND * BLOCK
    reach = (BAND - 1) * BLOCK
    halo_rows = halo_key.shape[0]
    query_doc = halo_doc[reach:].reshape(blocks, BLOCK, 1)
    key_doc = jnp.stack(
        [halo_doc[b * BLOCK : b * BLOCK + window_rows] for b in range(blocks)]
    ).reshape(blocks, 1, window_rows)
    block_spec = pl.BlockSpec((1, BLOCK, width), lambda b, slot: (b, 0, 0))
    whole = pl.BlockSpec((halo_rows, HEAD_DIM), lambda b, slot: (0, 0))
    grid_spec = pltpu.PrefetchScalarGridSpec(
        num_scalar_prefetch=1,
        grid=(blocks,),
        in_specs=[
            pl.BlockSpec((1, BLOCK, 1), lambda b, slot: (b, 0, 0)),
            pl.BlockSpec((1, 1, window_rows), lambda b, slot: (b, 0, 0)),
            block_spec,
            block_spec,
            whole,
            whole,
        ],
        out_specs=[
            pl.BlockSpec((1, BLOCK, 2 * width), lambda b, slot: (slot[b], 0, 0)),
            whole,
            whole,
        ],
    )
    return pl.pallas_call(
        fused_kernel,
        grid_spec=grid_spec,
        out_shape=[
            jax.ShapeDtypeStruct((slot_count, BLOCK, 2 * width), jnp.bfloat16),
            jax.ShapeDtypeStruct((halo_rows, HEAD_DIM), jnp.float32),
            jax.ShapeDtypeStruct((halo_rows, HEAD_DIM), jnp.float32),
        ],
        compiler_params=pltpu.CompilerParams(dimension_semantics=("arbitrary",)),
    )(slots, query_doc, key_doc, query_blocks, grad_blocks, halo_key, halo_value)


def shift_from_below(x, ctx_count, distance):
    pairs = [(s, s + distance) for s in range(ctx_count - distance)]
    return lax.ppermute(x, "ctx", pairs)


def shift_to_below(x, ctx_count, distance):
    pairs = [(s + distance, s) for s in range(ctx_count - distance)]
    return lax.ppermute(x, "ctx", pairs)


def on_device(queries, key_rows, value_rows, out_grad, doc_ids, block_owner):
    ctx_count = lax.axis_size("ctx")
    tp_count = lax.axis_size("tp")
    ctx_rank = lax.axis_index("ctx")
    local_rows, width = queries.shape
    head_cols = width // tp_count
    chunk_cols = head_cols // CHUNKS
    tok_dev = key_rows.shape[0]
    kv_cols = key_rows.shape[1]
    blocks_here = tok_dev // BLOCK
    reach = (BAND - 1) * BLOCK
    far = reach - tok_dev
    own_targets, held_sources = routing(block_owner, ctx_count, ctx_rank, blocks_here)
    kv_here = jnp.concatenate([key_rows, value_rows], axis=1)
    kv_near = shift_from_below(kv_here, ctx_count, 1)
    kv_far = shift_from_below(kv_here[tok_dev - far :], ctx_count, 2)
    halo = jnp.concatenate([kv_far, kv_near, kv_here], axis=0)
    halo_key = halo[:, :kv_cols]
    halo_value = halo[:, kv_cols:]
    padded_doc = jnp.concatenate([jnp.full((reach,), -1, doc_ids.dtype), doc_ids])
    halo_doc = lax.dynamic_slice_in_dim(padded_doc, ctx_rank * tok_dev, reach + tok_dev, 0)
    query_parts = queries.reshape(local_rows, tp_count, CHUNKS, chunk_cols)
    grad_parts = out_grad.reshape(local_rows, tp_count, CHUNKS, chunk_cols)
    held_parts = []
    key_grad = None
    for chunk in range(CHUNKS):
        both = jnp.concatenate([query_parts[:, :, chunk], grad_parts[:, :, chunk]], axis=-1)
        both = lax.all_to_all(both, "tp", split_axis=1, concat_axis=0, tiled=True)
        both = both.reshape(blocks_here, BLOCK, 2 * chunk_cols)
        results, chunk_key_grad, chunk_value_grad = fused_attention(
            own_targets,
            both[..., :chunk_cols],
            both[..., chunk_cols:],
            halo_key,
            halo_value,
            halo_doc,
            ctx_count,
        )
        if key_grad is None:
            key_grad, value_grad = chunk_key_grad, chunk_value_grad
        else:
            key_grad = key_grad + chunk_key_grad
            value_grad = value_grad + chunk_value_grad
        sent = lax.all_to_all(results, "ctx", split_axis=0, concat_axis=0, tiled=True)
        held_parts.append(jnp.take(sent, held_sources, axis=0))
    kv_grad = jnp.concatenate([key_grad, value_grad], axis=1)
    grad_near = shift_to_below(kv_grad[far:reach], ctx_count, 1)
    grad_far = shift_to_below(kv_grad[:far], ctx_count, 2)
    kv_total = kv_grad[reach:] + grad_near
    kv_total = kv_total.at[tok_dev - far :].add(grad_far)
    held_out = jnp.concatenate([part[..., :chunk_cols] for part in held_parts], axis=-1)
    held_dq = jnp.concatenate([part[..., chunk_cols:] for part in held_parts], axis=-1)
    return (
        held_out.reshape(tok_dev, head_cols),
        held_dq.reshape(tok_dev, head_cols),
        kv_total[:, :kv_cols].astype(jnp.bfloat16),
        kv_total[:, kv_cols:].astype(jnp.bfloat16),
    )


def solution(mesh):
    return jax.shard_map(
        on_device,
        mesh=mesh,
        in_specs=(
            P(("ctx", "tp"), None),
            P("ctx", "tp"),
            P("ctx", "tp"),
            P(("ctx", "tp"), None),
            P(),
            P(),
        ),
        out_specs=(P("ctx", "tp"), P("ctx", "tp"), P("ctx", "tp"), P("ctx", "tp")),
        check_vma=False,
    )
```

```python
import jax
import jax.numpy as jnp
from jax import lax
from jax.sharding import PartitionSpec as P
from jax.experimental import pallas as pl
from jax.experimental.pallas import tpu as pltpu

HEADS = 64
KV_HEADS = 8
HEAD_DIM = 128
BLOCK = 128
BAND = 12
CHUNKS = 2


def routing(block_owner, ctx_count, ctx_rank, blocks_here):
    owner_grid = block_owner.reshape(ctx_count, blocks_here)
    own_targets = lax.dynamic_index_in_dim(owner_grid, ctx_rank, 0, keepdims=False)
    sources = jnp.arange(ctx_count, dtype=jnp.int32)
    present = jnp.sum((owner_grid == ctx_rank).astype(jnp.int32), axis=1)
    arrival_rank = jnp.cumsum(present) - 1
    slot_index = jnp.arange(blocks_here, dtype=jnp.int32)
    chosen = (present[None, :] == 1) & (arrival_rank[None, :] == slot_index[:, None])
    held_sources = jnp.sum(chosen.astype(jnp.int32) * sources[None, :], axis=1)
    return (own_targets, held_sources)


def select_rows(selector, blocks):
    picked = jnp.einsum("ab,brh->arh", selector, blocks, preferred_element_type=jnp.float32)
    return picked.astype(jnp.bfloat16)


def halo_docs(doc_ids, first_row, halo_rows):
    positions = first_row + jnp.arange(halo_rows, dtype=jnp.int32)
    picked = jnp.take(doc_ids, jnp.clip(positions, 0, doc_ids.shape[0] - 1), axis=0)
    return jnp.where(positions >= 0, picked, -1)


def masked_scores(query_block, key_window, query_doc, key_doc, local_block):
    window_rows = key_window.shape[0]
    kv_local = key_window.shape[1]
    query_heads = query_block.reshape(BLOCK, kv_local, HEADS // KV_HEADS, HEAD_DIM)
    raw_scores = jnp.einsum(
        "qkgd,wkd->kgqw", query_heads, key_window, preferred_element_type=jnp.float32
    ) * HEAD_DIM ** (-0.5)
    query_pos = (BAND - 1) * BLOCK + jnp.arange(BLOCK, dtype=jnp.int32)
    key_pos = jnp.arange(window_rows, dtype=jnp.int32)
    allowed = (query_doc[:, None] == key_doc[None, :]) & (key_pos[None, :] <= query_pos[:, None])
    return (jnp.where(allowed[None, None], raw_scores, -1e30), query_heads)


def window_of(halo_key, halo_value, halo_doc, local_block):
    window_rows = BAND * BLOCK
    kv_local = halo_key.shape[1] // HEAD_DIM
    start = local_block * BLOCK
    key_window = lax.dynamic_slice_in_dim(halo_key, start, window_rows, 0)
    value_window = lax.dynamic_slice_in_dim(halo_value, start, window_rows, 0)
    key_doc = lax.dynamic_slice_in_dim(halo_doc, start, window_rows, 0)
    query_doc = lax.dynamic_slice_in_dim(halo_doc, start + (BAND - 1) * BLOCK, BLOCK, 0)
    return (
        key_window.reshape(window_rows, kv_local, HEAD_DIM),
        value_window.reshape(window_rows, kv_local, HEAD_DIM),
        query_doc,
        key_doc,
    )


def attend_forward(query_blocks, halo_key, halo_value, halo_doc):

    def advance(running, inputs):
        query_block, local_block = inputs
        key_window, value_window, query_doc, key_doc = window_of(
            halo_key, halo_value, halo_doc, local_block
        )
        scores, _ = masked_scores(query_block, key_window, query_doc, key_doc, local_block)
        row_max = jnp.max(scores, axis=-1, keepdims=True)
        log_total = row_max + jnp.log(jnp.sum(jnp.exp(scores - row_max), axis=-1, keepdims=True))
        soft_low = jnp.exp(scores - log_total).astype(jnp.bfloat16)
        natural_out = jnp.einsum(
            "kgqw,wkd->qkgd", soft_low, value_window, preferred_element_type=jnp.float32
        )
        return (running, (natural_out.reshape(BLOCK, -1).astype(jnp.bfloat16), log_total))

    local_ids = jnp.arange(query_blocks.shape[0], dtype=jnp.int32)
    _, (out_blocks, log_totals) = lax.scan(
        advance, jnp.zeros((), jnp.float32), (query_blocks, local_ids)
    )
    return (out_blocks, log_totals)


def attend_backward(query_blocks, grad_blocks, out_blocks, log_totals, halo_key, halo_value, halo_doc):
    window_rows = BAND * BLOCK
    inv_root = HEAD_DIM ** (-0.5)

    def advance(running, inputs):
        key_grad, value_grad = running
        query_block, grad_block, out_block, log_total, local_block = inputs
        key_window, value_window, query_doc, key_doc = window_of(
            halo_key, halo_value, halo_doc, local_block
        )
        scores, query_heads = masked_scores(
            query_block, key_window, query_doc, key_doc, local_block
        )
        grad_heads = grad_block.reshape(query_heads.shape)
        out_heads = out_block.reshape(query_heads.shape)
        weights = jnp.exp(scores - log_total)
        soft_low = weights.astype(jnp.bfloat16)
        row_dot = jnp.sum(grad_heads.astype(jnp.float32) * out_heads.astype(jnp.float32), axis=-1)
        row_dot = jnp.transpose(row_dot, (1, 2, 0))[..., None]
        prob_grad = jnp.einsum(
            "qkgd,wkd->kgqw", grad_heads, value_window, preferred_element_type=jnp.float32
        )
        score_grad = (weights * (prob_grad - row_dot)).astype(jnp.bfloat16)
        query_part = (
            jnp.einsum("kgqw,wkd->qkgd", score_grad, key_window, preferred_element_type=jnp.float32)
            * inv_root
        )
        key_part = (
            jnp.einsum(
                "kgqw,qkgd->wkd", score_grad, query_heads, preferred_element_type=jnp.float32
            )
            * inv_root
        )
        value_part = jnp.einsum(
            "kgqw,qkgd->wkd", soft_low, grad_heads, preferred_element_type=jnp.float32
        )
        start = local_block * BLOCK
        old_keys = lax.dynamic_slice_in_dim(key_grad, start, window_rows, 0)
        old_values = lax.dynamic_slice_in_dim(value_grad, start, window_rows, 0)
        key_grad = lax.dynamic_update_slice_in_dim(
            key_grad, old_keys + key_part.reshape(window_rows, -1), start, 0
        )
        value_grad = lax.dynamic_update_slice_in_dim(
            value_grad, old_values + value_part.reshape(window_rows, -1), start, 0
        )
        return ((key_grad, value_grad), query_part.reshape(BLOCK, -1).astype(jnp.bfloat16))

    zero_grads = (
        jnp.zeros(halo_key.shape, jnp.float32),
        jnp.zeros(halo_value.shape, jnp.float32),
    )
    local_ids = jnp.arange(query_blocks.shape[0], dtype=jnp.int32)
    (key_grad, value_grad), dq_blocks = lax.scan(
        advance, zero_grads, (query_blocks, grad_blocks, out_blocks, log_totals, local_ids)
    )
    return (dq_blocks, key_grad, value_grad)


TRANS_B = (((1,), (1,)), ((), ()))
TRANS_A = (((0,), (0,)), ((), ()))


def fused_kernel(slot_ref, qdoc_ref, kdoc_ref, q_ref, do_ref, k_ref, v_ref, res_ref, dk_ref, dv_ref):
    block = pl.program_id(0)
    window_rows = BAND * BLOCK
    scale = HEAD_DIM ** (-0.5)
    width = q_ref.shape[2]
    heads_here = width // HEAD_DIM

    @pl.when(block == 0)
    def _():
        dk_ref[...] = jnp.zeros_like(dk_ref)
        dv_ref[...] = jnp.zeros_like(dv_ref)

    start = pl.multiple_of(block * BLOCK, BLOCK)
    key_window = k_ref[pl.ds(start, window_rows), :]
    value_window = v_ref[pl.ds(start, window_rows), :]
    shape = (BLOCK, window_rows)
    rows = lax.broadcasted_iota(jnp.int32, shape, 0) + (BAND - 1) * BLOCK
    cols = lax.broadcasted_iota(jnp.int32, shape, 1)
    allowed = (qdoc_ref[0] == kdoc_ref[0]) & (cols <= rows)
    bias = jnp.where(allowed, 0.0, -1e30).astype(jnp.float32)
    dk_sum = None
    for head in range(heads_here):
        cols_of = slice(head * HEAD_DIM, (head + 1) * HEAD_DIM)
        query = q_ref[0, :, cols_of]
        raw = lax.dot_general(query, key_window, TRANS_B, preferred_element_type=jnp.float32) * scale
        scores = raw + bias
        row_max = jnp.max(scores, axis=1, keepdims=True)
        log_total = row_max + jnp.log(jnp.sum(jnp.exp(scores - row_max), axis=1, keepdims=True))
        weights = jnp.exp(scores - log_total)
        soft_low = weights.astype(jnp.bfloat16)
        out = jnp.dot(soft_low, value_window, preferred_element_type=jnp.float32).astype(jnp.bfloat16)
        res_ref[0, :, cols_of] = out
        grad = do_ref[0, :, cols_of]
        row_dot = jnp.sum(grad.astype(jnp.float32) * out.astype(jnp.float32), axis=1, keepdims=True)
        prob_grad = lax.dot_general(grad, value_window, TRANS_B, preferred_element_type=jnp.float32)
        score_grad = (weights * (prob_grad - row_dot)).astype(jnp.bfloat16)
        dq = jnp.dot(score_grad, key_window, preferred_element_type=jnp.float32) * scale
        res_ref[0, :, width + head * HEAD_DIM : width + (head + 1) * HEAD_DIM] = dq.astype(
            jnp.bfloat16
        )
        dk = lax.dot_general(score_grad, query, TRANS_A, preferred_element_type=jnp.float32) * scale
        dv = lax.dot_general(soft_low, grad, TRANS_A, preferred_element_type=jnp.float32)
        if dk_sum is None:
            dk_sum, dv_sum = dk, dv
        else:
            dk_sum, dv_sum = dk_sum + dk, dv_sum + dv
    dk_ref[pl.ds(start, window_rows), :] += dk_sum
    dv_ref[pl.ds(start, window_rows), :] += dv_sum


def fused_attention(slots, query_blocks, grad_blocks, halo_key, halo_value, halo_doc, slot_count):
    blocks, _, width = query_blocks.shape
    window_rows = BAND * BLOCK
    reach = (BAND - 1) * BLOCK
    halo_rows = halo_key.shape[0]
    query_doc = halo_doc[reach:].reshape(blocks, BLOCK, 1)
    key_doc = jnp.stack(
        [halo_doc[b * BLOCK : b * BLOCK + window_rows] for b in range(blocks)]
    ).reshape(blocks, 1, window_rows)
    block_spec = pl.BlockSpec((1, BLOCK, width), lambda b, slot: (b, 0, 0))
    whole = pl.BlockSpec((halo_rows, HEAD_DIM), lambda b, slot: (0, 0))
    grid_spec = pltpu.PrefetchScalarGridSpec(
        num_scalar_prefetch=1,
        grid=(blocks,),
        in_specs=[
            pl.BlockSpec((1, BLOCK, 1), lambda b, slot: (b, 0, 0)),
            pl.BlockSpec((1, 1, window_rows), lambda b, slot: (b, 0, 0)),
            block_spec,
            block_spec,
            whole,
            whole,
        ],
        out_specs=[
            pl.BlockSpec((1, BLOCK, 2 * width), lambda b, slot: (slot[b], 0, 0)),
            whole,
            whole,
        ],
    )
    return pl.pallas_call(
        fused_kernel,
        grid_spec=grid_spec,
        out_shape=[
            jax.ShapeDtypeStruct((slot_count, BLOCK, 2 * width), jnp.bfloat16),
            jax.ShapeDtypeStruct((halo_rows, HEAD_DIM), jnp.float32),
            jax.ShapeDtypeStruct((halo_rows, HEAD_DIM), jnp.float32),
        ],
        compiler_params=pltpu.CompilerParams(dimension_semantics=("arbitrary",)),
    )(slots, query_doc, key_doc, query_blocks, grad_blocks, halo_key, halo_value)


def shift_from_below(x, ctx_count, distance):
    pairs = [(s, s + distance) for s in range(ctx_count - distance)]
    return lax.ppermute(x, "ctx", pairs)


def shift_to_below(x, ctx_count, distance):
    pairs = [(s + distance, s) for s in range(ctx_count - distance)]
    return lax.ppermute(x, "ctx", pairs)


def on_device(queries, key_rows, value_rows, out_grad, doc_ids, block_owner):
    ctx_count = lax.axis_size("ctx")
    tp_count = lax.axis_size("tp")
    ctx_rank = lax.axis_index("ctx")
    local_rows, width = queries.shape
    head_cols = width // tp_count
    chunk_cols = head_cols // CHUNKS
    tok_dev = key_rows.shape[0]
    kv_cols = key_rows.shape[1]
    blocks_here = tok_dev // BLOCK
    reach = (BAND - 1) * BLOCK
    far = reach - tok_dev
    own_targets, held_sources = routing(block_owner, ctx_count, ctx_rank, blocks_here)
    kv_here = jnp.concatenate([key_rows, value_rows], axis=1)
    kv_near = shift_from_below(kv_here, ctx_count, 1)
    kv_far = shift_from_below(kv_here[tok_dev - far :], ctx_count, 2)
    halo = jnp.concatenate([kv_far, kv_near, kv_here], axis=0)
    halo_key = halo[:, :kv_cols]
    halo_value = halo[:, kv_cols:]
    padded_doc = jnp.concatenate([jnp.full((reach,), -1, doc_ids.dtype), doc_ids])
    halo_doc = lax.dynamic_slice_in_dim(padded_doc, ctx_rank * tok_dev, reach + tok_dev, 0)
    query_parts = queries.reshape(local_rows, tp_count, CHUNKS, chunk_cols)
    grad_parts = out_grad.reshape(local_rows, tp_count, CHUNKS, chunk_cols)
    held_parts = []
    key_grad = None
    for chunk in range(CHUNKS):
        both = jnp.concatenate([query_parts[:, :, chunk], grad_parts[:, :, chunk]], axis=-1)
        if chunk > 0:
            both, _ = lax.optimization_barrier((both, halo))
        both = lax.all_to_all(both, "tp", split_axis=1, concat_axis=0, tiled=True)
        both = both.reshape(blocks_here, BLOCK, 2 * chunk_cols)
        results, chunk_key_grad, chunk_value_grad = fused_attention(
            own_targets,
            both[..., :chunk_cols],
            both[..., chunk_cols:],
            halo_key,
            halo_value,
            halo_doc,
            ctx_count,
        )
        if key_grad is None:
            key_grad, value_grad = chunk_key_grad, chunk_value_grad
        else:
            key_grad = key_grad + chunk_key_grad
            value_grad = value_grad + chunk_value_grad
        sent = lax.all_to_all(results, "ctx", split_axis=0, concat_axis=0, tiled=True)
        held_parts.append(jnp.take(sent, held_sources, axis=0))
    kv_grad = jnp.concatenate([key_grad, value_grad], axis=1)
    grad_near = shift_to_below(kv_grad[far:reach], ctx_count, 1)
    grad_far = shift_to_below(kv_grad[:far], ctx_count, 2)
    kv_total = kv_grad[reach:] + grad_near
    kv_total = kv_total.at[tok_dev - far :].add(grad_far)
    held_out = jnp.concatenate([part[..., :chunk_cols] for part in held_parts], axis=-1)
    held_dq = jnp.concatenate([part[..., chunk_cols:] for part in held_parts], axis=-1)
    return (
        held_out.reshape(tok_dev, head_cols),
        held_dq.reshape(tok_dev, head_cols),
        kv_total[:, :kv_cols].astype(jnp.bfloat16),
        kv_total[:, kv_cols:].astype(jnp.bfloat16),
    )


def solution(mesh):
    return jax.shard_map(
        on_device,
        mesh=mesh,
        in_specs=(
            P(("ctx", "tp"), None),
            P("ctx", "tp"),
            P("ctx", "tp"),
            P(("ctx", "tp"), None),
            P(),
            P(),
        ),
        out_specs=(P("ctx", "tp"), P("ctx", "tp"), P("ctx", "tp"), P("ctx", "tp")),
        check_vma=False,
    )
```

```python
import jax
import jax.numpy as jnp
from jax import lax
from jax.sharding import PartitionSpec as P
from jax.experimental import pallas as pl
from jax.experimental.pallas import tpu as pltpu

HEADS = 64
KV_HEADS = 8
HEAD_DIM = 128
BLOCK = 128
BAND = 12
FIRST_SHARE = 3


def routing(block_owner, ctx_count, ctx_rank, blocks_here):
    owner_grid = block_owner.reshape(ctx_count, blocks_here)
    own_targets = lax.dynamic_index_in_dim(owner_grid, ctx_rank, 0, keepdims=False)
    sources = jnp.arange(ctx_count, dtype=jnp.int32)
    present = jnp.sum((owner_grid == ctx_rank).astype(jnp.int32), axis=1)
    arrival_rank = jnp.cumsum(present) - 1
    slot_index = jnp.arange(blocks_here, dtype=jnp.int32)
    chosen = (present[None, :] == 1) & (arrival_rank[None, :] == slot_index[:, None])
    held_sources = jnp.sum(chosen.astype(jnp.int32) * sources[None, :], axis=1)
    return (own_targets, held_sources)


def select_rows(selector, blocks):
    picked = jnp.einsum("ab,brh->arh", selector, blocks, preferred_element_type=jnp.float32)
    return picked.astype(jnp.bfloat16)


def halo_docs(doc_ids, first_row, halo_rows):
    positions = first_row + jnp.arange(halo_rows, dtype=jnp.int32)
    picked = jnp.take(doc_ids, jnp.clip(positions, 0, doc_ids.shape[0] - 1), axis=0)
    return jnp.where(positions >= 0, picked, -1)


def masked_scores(query_block, key_window, query_doc, key_doc, local_block):
    window_rows = key_window.shape[0]
    kv_local = key_window.shape[1]
    query_heads = query_block.reshape(BLOCK, kv_local, HEADS // KV_HEADS, HEAD_DIM)
    raw_scores = jnp.einsum(
        "qkgd,wkd->kgqw", query_heads, key_window, preferred_element_type=jnp.float32
    ) * HEAD_DIM ** (-0.5)
    query_pos = (BAND - 1) * BLOCK + jnp.arange(BLOCK, dtype=jnp.int32)
    key_pos = jnp.arange(window_rows, dtype=jnp.int32)
    allowed = (query_doc[:, None] == key_doc[None, :]) & (key_pos[None, :] <= query_pos[:, None])
    return (jnp.where(allowed[None, None], raw_scores, -1e30), query_heads)


def window_of(halo_key, halo_value, halo_doc, local_block):
    window_rows = BAND * BLOCK
    kv_local = halo_key.shape[1] // HEAD_DIM
    start = local_block * BLOCK
    key_window = lax.dynamic_slice_in_dim(halo_key, start, window_rows, 0)
    value_window = lax.dynamic_slice_in_dim(halo_value, start, window_rows, 0)
    key_doc = lax.dynamic_slice_in_dim(halo_doc, start, window_rows, 0)
    query_doc = lax.dynamic_slice_in_dim(halo_doc, start + (BAND - 1) * BLOCK, BLOCK, 0)
    return (
        key_window.reshape(window_rows, kv_local, HEAD_DIM),
        value_window.reshape(window_rows, kv_local, HEAD_DIM),
        query_doc,
        key_doc,
    )


def attend_forward(query_blocks, halo_key, halo_value, halo_doc):

    def advance(running, inputs):
        query_block, local_block = inputs
        key_window, value_window, query_doc, key_doc = window_of(
            halo_key, halo_value, halo_doc, local_block
        )
        scores, _ = masked_scores(query_block, key_window, query_doc, key_doc, local_block)
        row_max = jnp.max(scores, axis=-1, keepdims=True)
        log_total = row_max + jnp.log(jnp.sum(jnp.exp(scores - row_max), axis=-1, keepdims=True))
        soft_low = jnp.exp(scores - log_total).astype(jnp.bfloat16)
        natural_out = jnp.einsum(
            "kgqw,wkd->qkgd", soft_low, value_window, preferred_element_type=jnp.float32
        )
        return (running, (natural_out.reshape(BLOCK, -1).astype(jnp.bfloat16), log_total))

    local_ids = jnp.arange(query_blocks.shape[0], dtype=jnp.int32)
    _, (out_blocks, log_totals) = lax.scan(
        advance, jnp.zeros((), jnp.float32), (query_blocks, local_ids)
    )
    return (out_blocks, log_totals)


def attend_backward(query_blocks, grad_blocks, out_blocks, log_totals, halo_key, halo_value, halo_doc):
    window_rows = BAND * BLOCK
    inv_root = HEAD_DIM ** (-0.5)

    def advance(running, inputs):
        key_grad, value_grad = running
        query_block, grad_block, out_block, log_total, local_block = inputs
        key_window, value_window, query_doc, key_doc = window_of(
            halo_key, halo_value, halo_doc, local_block
        )
        scores, query_heads = masked_scores(
            query_block, key_window, query_doc, key_doc, local_block
        )
        grad_heads = grad_block.reshape(query_heads.shape)
        out_heads = out_block.reshape(query_heads.shape)
        weights = jnp.exp(scores - log_total)
        soft_low = weights.astype(jnp.bfloat16)
        row_dot = jnp.sum(grad_heads.astype(jnp.float32) * out_heads.astype(jnp.float32), axis=-1)
        row_dot = jnp.transpose(row_dot, (1, 2, 0))[..., None]
        prob_grad = jnp.einsum(
            "qkgd,wkd->kgqw", grad_heads, value_window, preferred_element_type=jnp.float32
        )
        score_grad = (weights * (prob_grad - row_dot)).astype(jnp.bfloat16)
        query_part = (
            jnp.einsum("kgqw,wkd->qkgd", score_grad, key_window, preferred_element_type=jnp.float32)
            * inv_root
        )
        key_part = (
            jnp.einsum(
                "kgqw,qkgd->wkd", score_grad, query_heads, preferred_element_type=jnp.float32
            )
            * inv_root
        )
        value_part = jnp.einsum(
            "kgqw,qkgd->wkd", soft_low, grad_heads, preferred_element_type=jnp.float32
        )
        start = local_block * BLOCK
        old_keys = lax.dynamic_slice_in_dim(key_grad, start, window_rows, 0)
        old_values = lax.dynamic_slice_in_dim(value_grad, start, window_rows, 0)
        key_grad = lax.dynamic_update_slice_in_dim(
            key_grad, old_keys + key_part.reshape(window_rows, -1), start, 0
        )
        value_grad = lax.dynamic_update_slice_in_dim(
            value_grad, old_values + value_part.reshape(window_rows, -1), start, 0
        )
        return ((key_grad, value_grad), query_part.reshape(BLOCK, -1).astype(jnp.bfloat16))

    zero_grads = (
        jnp.zeros(halo_key.shape, jnp.float32),
        jnp.zeros(halo_value.shape, jnp.float32),
    )
    local_ids = jnp.arange(query_blocks.shape[0], dtype=jnp.int32)
    (key_grad, value_grad), dq_blocks = lax.scan(
        advance, zero_grads, (query_blocks, grad_blocks, out_blocks, log_totals, local_ids)
    )
    return (dq_blocks, key_grad, value_grad)


TRANS_B = (((1,), (1,)), ((), ()))
TRANS_A = (((0,), (0,)), ((), ()))


def fused_kernel(slot_ref, qdoc_ref, kdoc_ref, q_ref, do_ref, k_ref, v_ref, res_ref, dk_ref, dv_ref):
    block = pl.program_id(0)
    window_rows = BAND * BLOCK
    scale = HEAD_DIM ** (-0.5)
    width = q_ref.shape[2]
    heads_here = width // HEAD_DIM

    @pl.when(block == 0)
    def _():
        dk_ref[...] = jnp.zeros_like(dk_ref)
        dv_ref[...] = jnp.zeros_like(dv_ref)

    start = pl.multiple_of(block * BLOCK, BLOCK)
    key_window = k_ref[pl.ds(start, window_rows), :]
    value_window = v_ref[pl.ds(start, window_rows), :]
    shape = (BLOCK, window_rows)
    rows = lax.broadcasted_iota(jnp.int32, shape, 0) + (BAND - 1) * BLOCK
    cols = lax.broadcasted_iota(jnp.int32, shape, 1)
    allowed = (qdoc_ref[0] == kdoc_ref[0]) & (cols <= rows)
    bias = jnp.where(allowed, 0.0, -1e30).astype(jnp.float32)
    dk_sum = None
    for head in range(heads_here):
        cols_of = slice(head * HEAD_DIM, (head + 1) * HEAD_DIM)
        query = q_ref[0, :, cols_of]
        raw = lax.dot_general(query, key_window, TRANS_B, preferred_element_type=jnp.float32) * scale
        scores = raw + bias
        row_max = jnp.max(scores, axis=1, keepdims=True)
        log_total = row_max + jnp.log(jnp.sum(jnp.exp(scores - row_max), axis=1, keepdims=True))
        weights = jnp.exp(scores - log_total)
        soft_low = weights.astype(jnp.bfloat16)
        out = jnp.dot(soft_low, value_window, preferred_element_type=jnp.float32).astype(jnp.bfloat16)
        res_ref[0, :, cols_of] = out
        grad = do_ref[0, :, cols_of]
        row_dot = jnp.sum(grad.astype(jnp.float32) * out.astype(jnp.float32), axis=1, keepdims=True)
        prob_grad = lax.dot_general(grad, value_window, TRANS_B, preferred_element_type=jnp.float32)
        score_grad = (weights * (prob_grad - row_dot)).astype(jnp.bfloat16)
        dq = jnp.dot(score_grad, key_window, preferred_element_type=jnp.float32) * scale
        res_ref[0, :, width + head * HEAD_DIM : width + (head + 1) * HEAD_DIM] = dq.astype(
            jnp.bfloat16
        )
        dk = lax.dot_general(score_grad, query, TRANS_A, preferred_element_type=jnp.float32) * scale
        dv = lax.dot_general(soft_low, grad, TRANS_A, preferred_element_type=jnp.float32)
        if dk_sum is None:
            dk_sum, dv_sum = dk, dv
        else:
            dk_sum, dv_sum = dk_sum + dk, dv_sum + dv
    dk_ref[pl.ds(start, window_rows), :] += dk_sum
    dv_ref[pl.ds(start, window_rows), :] += dv_sum


def fused_attention(slots, query_blocks, grad_blocks, halo_key, halo_value, halo_doc, slot_count):
    blocks, _, width = query_blocks.shape
    window_rows = BAND * BLOCK
    reach = (BAND - 1) * BLOCK
    halo_rows = halo_key.shape[0]
    query_doc = halo_doc[reach:].reshape(blocks, BLOCK, 1)
    key_doc = jnp.stack(
        [halo_doc[b * BLOCK : b * BLOCK + window_rows] for b in range(blocks)]
    ).reshape(blocks, 1, window_rows)
    block_spec = pl.BlockSpec((1, BLOCK, width), lambda b, slot: (b, 0, 0))
    whole = pl.BlockSpec((halo_rows, HEAD_DIM), lambda b, slot: (0, 0))
    grid_spec = pltpu.PrefetchScalarGridSpec(
        num_scalar_prefetch=1,
        grid=(blocks,),
        in_specs=[
            pl.BlockSpec((1, BLOCK, 1), lambda b, slot: (b, 0, 0)),
            pl.BlockSpec((1, 1, window_rows), lambda b, slot: (b, 0, 0)),
            block_spec,
            block_spec,
            whole,
            whole,
        ],
        out_specs=[
            pl.BlockSpec((1, BLOCK, 2 * width), lambda b, slot: (slot[b], 0, 0)),
            whole,
            whole,
        ],
    )
    return pl.pallas_call(
        fused_kernel,
        grid_spec=grid_spec,
        out_shape=[
            jax.ShapeDtypeStruct((slot_count, BLOCK, 2 * width), jnp.bfloat16),
            jax.ShapeDtypeStruct((halo_rows, HEAD_DIM), jnp.float32),
            jax.ShapeDtypeStruct((halo_rows, HEAD_DIM), jnp.float32),
        ],
        compiler_params=pltpu.CompilerParams(dimension_semantics=("arbitrary",)),
    )(slots, query_doc, key_doc, query_blocks, grad_blocks, halo_key, halo_value)


def shift_from_below(x, ctx_count, distance):
    pairs = [(s, s + distance) for s in range(ctx_count - distance)]
    return lax.ppermute(x, "ctx", pairs)


def shift_to_below(x, ctx_count, distance):
    pairs = [(s + distance, s) for s in range(ctx_count - distance)]
    return lax.ppermute(x, "ctx", pairs)


def on_device(queries, key_rows, value_rows, out_grad, doc_ids, block_owner):
    ctx_count = lax.axis_size("ctx")
    tp_count = lax.axis_size("tp")
    ctx_rank = lax.axis_index("ctx")
    local_rows, width = queries.shape
    head_cols = width // tp_count
    first_cols = (head_cols // HEAD_DIM) * FIRST_SHARE // 8 * HEAD_DIM
    bounds = [(0, first_cols), (first_cols, head_cols)]
    tok_dev = key_rows.shape[0]
    kv_cols = key_rows.shape[1]
    blocks_here = tok_dev // BLOCK
    reach = (BAND - 1) * BLOCK
    far = reach - tok_dev
    own_targets, held_sources = routing(block_owner, ctx_count, ctx_rank, blocks_here)
    kv_here = jnp.concatenate([key_rows, value_rows], axis=1)
    kv_near = shift_from_below(kv_here, ctx_count, 1)
    kv_far = shift_from_below(kv_here[tok_dev - far :], ctx_count, 2)
    halo = jnp.concatenate([kv_far, kv_near, kv_here], axis=0)
    halo_key = halo[:, :kv_cols]
    halo_value = halo[:, kv_cols:]
    padded_doc = jnp.concatenate([jnp.full((reach,), -1, doc_ids.dtype), doc_ids])
    halo_doc = lax.dynamic_slice_in_dim(padded_doc, ctx_rank * tok_dev, reach + tok_dev, 0)
    query_parts = queries.reshape(local_rows, tp_count, head_cols)
    grad_parts = out_grad.reshape(local_rows, tp_count, head_cols)
    held_parts = []
    key_grad = None
    for chunk, (low, high) in enumerate(bounds):
        chunk_cols = high - low
        both = jnp.concatenate([query_parts[:, :, low:high], grad_parts[:, :, low:high]], axis=-1)
        if chunk > 0:
            both, _ = lax.optimization_barrier((both, halo))
        both = lax.all_to_all(both, "tp", split_axis=1, concat_axis=0, tiled=True)
        both = both.reshape(blocks_here, BLOCK, 2 * chunk_cols)
        results, chunk_key_grad, chunk_value_grad = fused_attention(
            own_targets,
            both[..., :chunk_cols],
            both[..., chunk_cols:],
            halo_key,
            halo_value,
            halo_doc,
            ctx_count,
        )
        if key_grad is None:
            key_grad, value_grad = chunk_key_grad, chunk_value_grad
        else:
            key_grad = key_grad + chunk_key_grad
            value_grad = value_grad + chunk_value_grad
        sent = lax.all_to_all(results, "ctx", split_axis=0, concat_axis=0, tiled=True)
        held_parts.append(jnp.take(sent, held_sources, axis=0))
    kv_grad = jnp.concatenate([key_grad, value_grad], axis=1)
    grad_near = shift_to_below(kv_grad[far:reach], ctx_count, 1)
    grad_far = shift_to_below(kv_grad[:far], ctx_count, 2)
    kv_total = kv_grad[reach:] + grad_near
    kv_total = kv_total.at[tok_dev - far :].add(grad_far)
    widths = [high - low for low, high in bounds]
    held_out = jnp.concatenate([p[..., :w] for p, w in zip(held_parts, widths)], axis=-1)
    held_dq = jnp.concatenate([p[..., w:] for p, w in zip(held_parts, widths)], axis=-1)
    return (
        held_out.reshape(tok_dev, head_cols),
        held_dq.reshape(tok_dev, head_cols),
        kv_total[:, :kv_cols].astype(jnp.bfloat16),
        kv_total[:, kv_cols:].astype(jnp.bfloat16),
    )


def solution(mesh):
    return jax.shard_map(
        on_device,
        mesh=mesh,
        in_specs=(
            P(("ctx", "tp"), None),
            P("ctx", "tp"),
            P("ctx", "tp"),
            P(("ctx", "tp"), None),
            P(),
            P(),
        ),
        out_specs=(P("ctx", "tp"), P("ctx", "tp"), P("ctx", "tp"), P("ctx", "tp")),
        check_vma=False,
    )
```

```python
import jax
import jax.numpy as jnp
from jax import lax
from jax.sharding import PartitionSpec as P
from jax.experimental import pallas as pl
from jax.experimental.pallas import tpu as pltpu

HEADS = 64
KV_HEADS = 8
HEAD_DIM = 128
BLOCK = 128
BAND = 12
FIRST_SHARE = 3


def routing(block_owner, ctx_count, ctx_rank, blocks_here):
    owner_grid = block_owner.reshape(ctx_count, blocks_here)
    own_targets = lax.dynamic_index_in_dim(owner_grid, ctx_rank, 0, keepdims=False)
    sources = jnp.arange(ctx_count, dtype=jnp.int32)
    present = jnp.sum((owner_grid == ctx_rank).astype(jnp.int32), axis=1)
    arrival_rank = jnp.cumsum(present) - 1
    slot_index = jnp.arange(blocks_here, dtype=jnp.int32)
    chosen = (present[None, :] == 1) & (arrival_rank[None, :] == slot_index[:, None])
    held_sources = jnp.sum(chosen.astype(jnp.int32) * sources[None, :], axis=1)
    return (own_targets, held_sources)


def select_rows(selector, blocks):
    picked = jnp.einsum("ab,brh->arh", selector, blocks, preferred_element_type=jnp.float32)
    return picked.astype(jnp.bfloat16)


def halo_docs(doc_ids, first_row, halo_rows):
    positions = first_row + jnp.arange(halo_rows, dtype=jnp.int32)
    picked = jnp.take(doc_ids, jnp.clip(positions, 0, doc_ids.shape[0] - 1), axis=0)
    return jnp.where(positions >= 0, picked, -1)


def masked_scores(query_block, key_window, query_doc, key_doc, local_block):
    window_rows = key_window.shape[0]
    kv_local = key_window.shape[1]
    query_heads = query_block.reshape(BLOCK, kv_local, HEADS // KV_HEADS, HEAD_DIM)
    raw_scores = jnp.einsum(
        "qkgd,wkd->kgqw", query_heads, key_window, preferred_element_type=jnp.float32
    ) * HEAD_DIM ** (-0.5)
    query_pos = (BAND - 1) * BLOCK + jnp.arange(BLOCK, dtype=jnp.int32)
    key_pos = jnp.arange(window_rows, dtype=jnp.int32)
    allowed = (query_doc[:, None] == key_doc[None, :]) & (key_pos[None, :] <= query_pos[:, None])
    return (jnp.where(allowed[None, None], raw_scores, -1e30), query_heads)


def window_of(halo_key, halo_value, halo_doc, local_block):
    window_rows = BAND * BLOCK
    kv_local = halo_key.shape[1] // HEAD_DIM
    start = local_block * BLOCK
    key_window = lax.dynamic_slice_in_dim(halo_key, start, window_rows, 0)
    value_window = lax.dynamic_slice_in_dim(halo_value, start, window_rows, 0)
    key_doc = lax.dynamic_slice_in_dim(halo_doc, start, window_rows, 0)
    query_doc = lax.dynamic_slice_in_dim(halo_doc, start + (BAND - 1) * BLOCK, BLOCK, 0)
    return (
        key_window.reshape(window_rows, kv_local, HEAD_DIM),
        value_window.reshape(window_rows, kv_local, HEAD_DIM),
        query_doc,
        key_doc,
    )


def attend_forward(query_blocks, halo_key, halo_value, halo_doc):

    def advance(running, inputs):
        query_block, local_block = inputs
        key_window, value_window, query_doc, key_doc = window_of(
            halo_key, halo_value, halo_doc, local_block
        )
        scores, _ = masked_scores(query_block, key_window, query_doc, key_doc, local_block)
        row_max = jnp.max(scores, axis=-1, keepdims=True)
        log_total = row_max + jnp.log(jnp.sum(jnp.exp(scores - row_max), axis=-1, keepdims=True))
        soft_low = jnp.exp(scores - log_total).astype(jnp.bfloat16)
        natural_out = jnp.einsum(
            "kgqw,wkd->qkgd", soft_low, value_window, preferred_element_type=jnp.float32
        )
        return (running, (natural_out.reshape(BLOCK, -1).astype(jnp.bfloat16), log_total))

    local_ids = jnp.arange(query_blocks.shape[0], dtype=jnp.int32)
    _, (out_blocks, log_totals) = lax.scan(
        advance, jnp.zeros((), jnp.float32), (query_blocks, local_ids)
    )
    return (out_blocks, log_totals)


def attend_backward(query_blocks, grad_blocks, out_blocks, log_totals, halo_key, halo_value, halo_doc):
    window_rows = BAND * BLOCK
    inv_root = HEAD_DIM ** (-0.5)

    def advance(running, inputs):
        key_grad, value_grad = running
        query_block, grad_block, out_block, log_total, local_block = inputs
        key_window, value_window, query_doc, key_doc = window_of(
            halo_key, halo_value, halo_doc, local_block
        )
        scores, query_heads = masked_scores(
            query_block, key_window, query_doc, key_doc, local_block
        )
        grad_heads = grad_block.reshape(query_heads.shape)
        out_heads = out_block.reshape(query_heads.shape)
        weights = jnp.exp(scores - log_total)
        soft_low = weights.astype(jnp.bfloat16)
        row_dot = jnp.sum(grad_heads.astype(jnp.float32) * out_heads.astype(jnp.float32), axis=-1)
        row_dot = jnp.transpose(row_dot, (1, 2, 0))[..., None]
        prob_grad = jnp.einsum(
            "qkgd,wkd->kgqw", grad_heads, value_window, preferred_element_type=jnp.float32
        )
        score_grad = (weights * (prob_grad - row_dot)).astype(jnp.bfloat16)
        query_part = (
            jnp.einsum("kgqw,wkd->qkgd", score_grad, key_window, preferred_element_type=jnp.float32)
            * inv_root
        )
        key_part = (
            jnp.einsum(
                "kgqw,qkgd->wkd", score_grad, query_heads, preferred_element_type=jnp.float32
            )
            * inv_root
        )
        value_part = jnp.einsum(
            "kgqw,qkgd->wkd", soft_low, grad_heads, preferred_element_type=jnp.float32
        )
        start = local_block * BLOCK
        old_keys = lax.dynamic_slice_in_dim(key_grad, start, window_rows, 0)
        old_values = lax.dynamic_slice_in_dim(value_grad, start, window_rows, 0)
        key_grad = lax.dynamic_update_slice_in_dim(
            key_grad, old_keys + key_part.reshape(window_rows, -1), start, 0
        )
        value_grad = lax.dynamic_update_slice_in_dim(
            value_grad, old_values + value_part.reshape(window_rows, -1), start, 0
        )
        return ((key_grad, value_grad), query_part.reshape(BLOCK, -1).astype(jnp.bfloat16))

    zero_grads = (
        jnp.zeros(halo_key.shape, jnp.float32),
        jnp.zeros(halo_value.shape, jnp.float32),
    )
    local_ids = jnp.arange(query_blocks.shape[0], dtype=jnp.int32)
    (key_grad, value_grad), dq_blocks = lax.scan(
        advance, zero_grads, (query_blocks, grad_blocks, out_blocks, log_totals, local_ids)
    )
    return (dq_blocks, key_grad, value_grad)


TRANS_B = (((1,), (1,)), ((), ()))
TRANS_A = (((0,), (0,)), ((), ()))


def fused_kernel(slot_ref, qdoc_ref, kdoc_ref, q_ref, do_ref, k_ref, v_ref, res_ref, dk_ref, dv_ref):
    block = pl.program_id(0)
    window_rows = BAND * BLOCK
    scale = HEAD_DIM ** (-0.5)
    width = q_ref.shape[2]
    heads_here = width // HEAD_DIM

    @pl.when(block == 0)
    def _():
        dk_ref[...] = jnp.zeros_like(dk_ref)
        dv_ref[...] = jnp.zeros_like(dv_ref)

    start = pl.multiple_of(block * BLOCK, BLOCK)
    key_window = k_ref[pl.ds(start, window_rows), :]
    value_window = v_ref[pl.ds(start, window_rows), :]
    shape = (BLOCK, window_rows)
    rows = lax.broadcasted_iota(jnp.int32, shape, 0) + (BAND - 1) * BLOCK
    cols = lax.broadcasted_iota(jnp.int32, shape, 1)
    allowed = (qdoc_ref[0] == kdoc_ref[0]) & (cols <= rows)
    bias = jnp.where(allowed, 0.0, -1e30).astype(jnp.float32)
    dk_sum = None
    for head in range(heads_here):
        cols_of = slice(head * HEAD_DIM, (head + 1) * HEAD_DIM)
        query = q_ref[0, :, cols_of]
        raw = lax.dot_general(query, key_window, TRANS_B, preferred_element_type=jnp.float32) * scale
        scores = raw + bias
        row_max = jnp.max(scores, axis=1, keepdims=True)
        shifted = jnp.exp(scores - row_max)
        weights = shifted * (1.0 / jnp.sum(shifted, axis=1, keepdims=True))
        soft_low = weights.astype(jnp.bfloat16)
        out = jnp.dot(soft_low, value_window, preferred_element_type=jnp.float32).astype(jnp.bfloat16)
        res_ref[0, :, cols_of] = out
        grad = do_ref[0, :, cols_of]
        row_dot = jnp.sum(grad.astype(jnp.float32) * out.astype(jnp.float32), axis=1, keepdims=True)
        prob_grad = lax.dot_general(grad, value_window, TRANS_B, preferred_element_type=jnp.float32)
        score_grad = (weights * (prob_grad - row_dot)).astype(jnp.bfloat16)
        dq = jnp.dot(score_grad, key_window, preferred_element_type=jnp.float32) * scale
        res_ref[0, :, width + head * HEAD_DIM : width + (head + 1) * HEAD_DIM] = dq.astype(
            jnp.bfloat16
        )
        dk = lax.dot_general(score_grad, query, TRANS_A, preferred_element_type=jnp.float32)
        dv = lax.dot_general(soft_low, grad, TRANS_A, preferred_element_type=jnp.float32)
        if dk_sum is None:
            dk_sum, dv_sum = dk, dv
        else:
            dk_sum, dv_sum = dk_sum + dk, dv_sum + dv
    dk_ref[pl.ds(start, window_rows), :] += dk_sum * scale
    dv_ref[pl.ds(start, window_rows), :] += dv_sum


def fused_attention(slots, query_blocks, grad_blocks, halo_key, halo_value, halo_doc, slot_count):
    blocks, _, width = query_blocks.shape
    window_rows = BAND * BLOCK
    reach = (BAND - 1) * BLOCK
    halo_rows = halo_key.shape[0]
    query_doc = halo_doc[reach:].reshape(blocks, BLOCK, 1)
    key_doc = jnp.stack(
        [halo_doc[b * BLOCK : b * BLOCK + window_rows] for b in range(blocks)]
    ).reshape(blocks, 1, window_rows)
    block_spec = pl.BlockSpec((1, BLOCK, width), lambda b, slot: (b, 0, 0))
    whole = pl.BlockSpec((halo_rows, HEAD_DIM), lambda b, slot: (0, 0))
    grid_spec = pltpu.PrefetchScalarGridSpec(
        num_scalar_prefetch=1,
        grid=(blocks,),
        in_specs=[
            pl.BlockSpec((1, BLOCK, 1), lambda b, slot: (b, 0, 0)),
            pl.BlockSpec((1, 1, window_rows), lambda b, slot: (b, 0, 0)),
            block_spec,
            block_spec,
            whole,
            whole,
        ],
        out_specs=[
            pl.BlockSpec((1, BLOCK, 2 * width), lambda b, slot: (slot[b], 0, 0)),
            whole,
            whole,
        ],
    )
    return pl.pallas_call(
        fused_kernel,
        grid_spec=grid_spec,
        out_shape=[
            jax.ShapeDtypeStruct((slot_count, BLOCK, 2 * width), jnp.bfloat16),
            jax.ShapeDtypeStruct((halo_rows, HEAD_DIM), jnp.float32),
            jax.ShapeDtypeStruct((halo_rows, HEAD_DIM), jnp.float32),
        ],
        compiler_params=pltpu.CompilerParams(dimension_semantics=("arbitrary",)),
    )(slots, query_doc, key_doc, query_blocks, grad_blocks, halo_key, halo_value)


def shift_from_below(x, ctx_count, distance):
    pairs = [(s, s + distance) for s in range(ctx_count - distance)]
    return lax.ppermute(x, "ctx", pairs)


def shift_to_below(x, ctx_count, distance):
    pairs = [(s + distance, s) for s in range(ctx_count - distance)]
    return lax.ppermute(x, "ctx", pairs)


def on_device(queries, key_rows, value_rows, out_grad, doc_ids, block_owner):
    ctx_count = lax.axis_size("ctx")
    tp_count = lax.axis_size("tp")
    ctx_rank = lax.axis_index("ctx")
    local_rows, width = queries.shape
    head_cols = width // tp_count
    first_cols = (head_cols // HEAD_DIM) * FIRST_SHARE // 8 * HEAD_DIM
    bounds = [(0, first_cols), (first_cols, head_cols)]
    tok_dev = key_rows.shape[0]
    kv_cols = key_rows.shape[1]
    blocks_here = tok_dev // BLOCK
    reach = (BAND - 1) * BLOCK
    far = reach - tok_dev
    own_targets, held_sources = routing(block_owner, ctx_count, ctx_rank, blocks_here)
    kv_here = jnp.concatenate([key_rows, value_rows], axis=1)
    kv_near = shift_from_below(kv_here, ctx_count, 1)
    kv_far = shift_from_below(kv_here[tok_dev - far :], ctx_count, 2)
    halo = jnp.concatenate([kv_far, kv_near, kv_here], axis=0)
    halo_key = halo[:, :kv_cols]
    halo_value = halo[:, kv_cols:]
    padded_doc = jnp.concatenate([jnp.full((reach,), -1, doc_ids.dtype), doc_ids])
    halo_doc = lax.dynamic_slice_in_dim(padded_doc, ctx_rank * tok_dev, reach + tok_dev, 0)
    query_parts = queries.reshape(local_rows, tp_count, head_cols)
    grad_parts = out_grad.reshape(local_rows, tp_count, head_cols)
    held_parts = []
    key_grad = None
    for chunk, (low, high) in enumerate(bounds):
        chunk_cols = high - low
        both = jnp.concatenate([query_parts[:, :, low:high], grad_parts[:, :, low:high]], axis=-1)
        if chunk > 0:
            both, _ = lax.optimization_barrier((both, halo))
        both = lax.all_to_all(both, "tp", split_axis=1, concat_axis=0, tiled=True)
        both = both.reshape(blocks_here, BLOCK, 2 * chunk_cols)
        results, chunk_key_grad, chunk_value_grad = fused_attention(
            own_targets,
            both[..., :chunk_cols],
            both[..., chunk_cols:],
            halo_key,
            halo_value,
            halo_doc,
            ctx_count,
        )
        if key_grad is None:
            key_grad, value_grad = chunk_key_grad, chunk_value_grad
        else:
            key_grad = key_grad + chunk_key_grad
            value_grad = value_grad + chunk_value_grad
        sent = lax.all_to_all(results, "ctx", split_axis=0, concat_axis=0, tiled=True)
        held_parts.append(jnp.take(sent, held_sources, axis=0))
    kv_grad = jnp.concatenate([key_grad, value_grad], axis=1)
    grad_near = shift_to_below(kv_grad[far:reach], ctx_count, 1)
    grad_far = shift_to_below(kv_grad[:far], ctx_count, 2)
    kv_total = kv_grad[reach:] + grad_near
    kv_total = kv_total.at[tok_dev - far :].add(grad_far)
    widths = [high - low for low, high in bounds]
    held_out = jnp.concatenate([p[..., :w] for p, w in zip(held_parts, widths)], axis=-1)
    held_dq = jnp.concatenate([p[..., w:] for p, w in zip(held_parts, widths)], axis=-1)
    return (
        held_out.reshape(tok_dev, head_cols),
        held_dq.reshape(tok_dev, head_cols),
        kv_total[:, :kv_cols].astype(jnp.bfloat16),
        kv_total[:, kv_cols:].astype(jnp.bfloat16),
    )


def solution(mesh):
    return jax.shard_map(
        on_device,
        mesh=mesh,
        in_specs=(
            P(("ctx", "tp"), None),
            P("ctx", "tp"),
            P("ctx", "tp"),
            P(("ctx", "tp"), None),
            P(),
            P(),
        ),
        out_specs=(P("ctx", "tp"), P("ctx", "tp"), P("ctx", "tp"), P("ctx", "tp")),
        check_vma=False,
    )
```

```python
import jax
import jax.numpy as jnp
from jax import lax
from jax.sharding import PartitionSpec as P
from jax.experimental import pallas as pl
from jax.experimental.pallas import tpu as pltpu

HEADS = 64
KV_HEADS = 8
HEAD_DIM = 128
BLOCK = 128
BAND = 12
FIRST_SHARE = 3


def routing(block_owner, ctx_count, ctx_rank, blocks_here):
    owner_grid = block_owner.reshape(ctx_count, blocks_here)
    own_targets = lax.dynamic_index_in_dim(owner_grid, ctx_rank, 0, keepdims=False)
    sources = jnp.arange(ctx_count, dtype=jnp.int32)
    present = jnp.sum((owner_grid == ctx_rank).astype(jnp.int32), axis=1)
    arrival_rank = jnp.cumsum(present) - 1
    slot_index = jnp.arange(blocks_here, dtype=jnp.int32)
    chosen = (present[None, :] == 1) & (arrival_rank[None, :] == slot_index[:, None])
    held_sources = jnp.sum(chosen.astype(jnp.int32) * sources[None, :], axis=1)
    return (own_targets, held_sources)


def select_rows(selector, blocks):
    picked = jnp.einsum("ab,brh->arh", selector, blocks, preferred_element_type=jnp.float32)
    return picked.astype(jnp.bfloat16)


def halo_docs(doc_ids, first_row, halo_rows):
    positions = first_row + jnp.arange(halo_rows, dtype=jnp.int32)
    picked = jnp.take(doc_ids, jnp.clip(positions, 0, doc_ids.shape[0] - 1), axis=0)
    return jnp.where(positions >= 0, picked, -1)


def masked_scores(query_block, key_window, query_doc, key_doc, local_block):
    window_rows = key_window.shape[0]
    kv_local = key_window.shape[1]
    query_heads = query_block.reshape(BLOCK, kv_local, HEADS // KV_HEADS, HEAD_DIM)
    raw_scores = jnp.einsum(
        "qkgd,wkd->kgqw", query_heads, key_window, preferred_element_type=jnp.float32
    ) * HEAD_DIM ** (-0.5)
    query_pos = (BAND - 1) * BLOCK + jnp.arange(BLOCK, dtype=jnp.int32)
    key_pos = jnp.arange(window_rows, dtype=jnp.int32)
    allowed = (query_doc[:, None] == key_doc[None, :]) & (key_pos[None, :] <= query_pos[:, None])
    return (jnp.where(allowed[None, None], raw_scores, -1e30), query_heads)


def window_of(halo_key, halo_value, halo_doc, local_block):
    window_rows = BAND * BLOCK
    kv_local = halo_key.shape[1] // HEAD_DIM
    start = local_block * BLOCK
    key_window = lax.dynamic_slice_in_dim(halo_key, start, window_rows, 0)
    value_window = lax.dynamic_slice_in_dim(halo_value, start, window_rows, 0)
    key_doc = lax.dynamic_slice_in_dim(halo_doc, start, window_rows, 0)
    query_doc = lax.dynamic_slice_in_dim(halo_doc, start + (BAND - 1) * BLOCK, BLOCK, 0)
    return (
        key_window.reshape(window_rows, kv_local, HEAD_DIM),
        value_window.reshape(window_rows, kv_local, HEAD_DIM),
        query_doc,
        key_doc,
    )


def attend_forward(query_blocks, halo_key, halo_value, halo_doc):

    def advance(running, inputs):
        query_block, local_block = inputs
        key_window, value_window, query_doc, key_doc = window_of(
            halo_key, halo_value, halo_doc, local_block
        )
        scores, _ = masked_scores(query_block, key_window, query_doc, key_doc, local_block)
        row_max = jnp.max(scores, axis=-1, keepdims=True)
        log_total = row_max + jnp.log(jnp.sum(jnp.exp(scores - row_max), axis=-1, keepdims=True))
        soft_low = jnp.exp(scores - log_total).astype(jnp.bfloat16)
        natural_out = jnp.einsum(
            "kgqw,wkd->qkgd", soft_low, value_window, preferred_element_type=jnp.float32
        )
        return (running, (natural_out.reshape(BLOCK, -1).astype(jnp.bfloat16), log_total))

    local_ids = jnp.arange(query_blocks.shape[0], dtype=jnp.int32)
    _, (out_blocks, log_totals) = lax.scan(
        advance, jnp.zeros((), jnp.float32), (query_blocks, local_ids)
    )
    return (out_blocks, log_totals)


def attend_backward(query_blocks, grad_blocks, out_blocks, log_totals, halo_key, halo_value, halo_doc):
    window_rows = BAND * BLOCK
    inv_root = HEAD_DIM ** (-0.5)

    def advance(running, inputs):
        key_grad, value_grad = running
        query_block, grad_block, out_block, log_total, local_block = inputs
        key_window, value_window, query_doc, key_doc = window_of(
            halo_key, halo_value, halo_doc, local_block
        )
        scores, query_heads = masked_scores(
            query_block, key_window, query_doc, key_doc, local_block
        )
        grad_heads = grad_block.reshape(query_heads.shape)
        out_heads = out_block.reshape(query_heads.shape)
        weights = jnp.exp(scores - log_total)
        soft_low = weights.astype(jnp.bfloat16)
        row_dot = jnp.sum(grad_heads.astype(jnp.float32) * out_heads.astype(jnp.float32), axis=-1)
        row_dot = jnp.transpose(row_dot, (1, 2, 0))[..., None]
        prob_grad = jnp.einsum(
            "qkgd,wkd->kgqw", grad_heads, value_window, preferred_element_type=jnp.float32
        )
        score_grad = (weights * (prob_grad - row_dot)).astype(jnp.bfloat16)
        query_part = (
            jnp.einsum("kgqw,wkd->qkgd", score_grad, key_window, preferred_element_type=jnp.float32)
            * inv_root
        )
        key_part = (
            jnp.einsum(
                "kgqw,qkgd->wkd", score_grad, query_heads, preferred_element_type=jnp.float32
            )
            * inv_root
        )
        value_part = jnp.einsum(
            "kgqw,qkgd->wkd", soft_low, grad_heads, preferred_element_type=jnp.float32
        )
        start = local_block * BLOCK
        old_keys = lax.dynamic_slice_in_dim(key_grad, start, window_rows, 0)
        old_values = lax.dynamic_slice_in_dim(value_grad, start, window_rows, 0)
        key_grad = lax.dynamic_update_slice_in_dim(
            key_grad, old_keys + key_part.reshape(window_rows, -1), start, 0
        )
        value_grad = lax.dynamic_update_slice_in_dim(
            value_grad, old_values + value_part.reshape(window_rows, -1), start, 0
        )
        return ((key_grad, value_grad), query_part.reshape(BLOCK, -1).astype(jnp.bfloat16))

    zero_grads = (
        jnp.zeros(halo_key.shape, jnp.float32),
        jnp.zeros(halo_value.shape, jnp.float32),
    )
    local_ids = jnp.arange(query_blocks.shape[0], dtype=jnp.int32)
    (key_grad, value_grad), dq_blocks = lax.scan(
        advance, zero_grads, (query_blocks, grad_blocks, out_blocks, log_totals, local_ids)
    )
    return (dq_blocks, key_grad, value_grad)


TRANS_B = (((1,), (1,)), ((), ()))
TRANS_A = (((0,), (0,)), ((), ()))


def fused_kernel(slot_ref, qdoc_ref, kdoc_ref, q_ref, do_ref, k_ref, v_ref, res_ref, dk_ref, dv_ref):
    block = pl.program_id(0)
    window_rows = BAND * BLOCK
    scale = HEAD_DIM ** (-0.5)
    width = q_ref.shape[2]
    heads_here = width // HEAD_DIM

    @pl.when(block == 0)
    def _():
        dk_ref[...] = jnp.zeros_like(dk_ref)
        dv_ref[...] = jnp.zeros_like(dv_ref)

    start = pl.multiple_of(block * BLOCK, BLOCK)
    key_window = k_ref[pl.ds(start, window_rows), :]
    value_window = v_ref[pl.ds(start, window_rows), :]
    shape = (BLOCK, window_rows)
    rows = lax.broadcasted_iota(jnp.int32, shape, 0) + (BAND - 1) * BLOCK
    cols = lax.broadcasted_iota(jnp.int32, shape, 1)
    allowed = (qdoc_ref[0] == kdoc_ref[0]) & (cols <= rows)
    bias = jnp.where(allowed, 0.0, -1e30).astype(jnp.float32)
    dk_sum = None
    for head in range(heads_here):
        cols_of = slice(head * HEAD_DIM, (head + 1) * HEAD_DIM)
        query = q_ref[0, :, cols_of]
        raw = lax.dot_general(query, key_window, TRANS_B, preferred_element_type=jnp.float32) * scale
        scores = raw + bias
        row_max = jnp.max(scores, axis=1, keepdims=True)
        shifted = jnp.exp(scores - row_max)
        weights = shifted * (1.0 / jnp.sum(shifted, axis=1, keepdims=True))
        soft_low = weights.astype(jnp.bfloat16)
        out = jnp.dot(soft_low, value_window, preferred_element_type=jnp.float32).astype(jnp.bfloat16)
        res_ref[0, :, cols_of] = out
        grad = do_ref[0, :, cols_of]
        row_dot = jnp.sum(grad.astype(jnp.float32) * out.astype(jnp.float32), axis=1, keepdims=True)
        prob_grad = lax.dot_general(grad, value_window, TRANS_B, preferred_element_type=jnp.float32)
        score_grad = (weights * (prob_grad - row_dot)).astype(jnp.bfloat16)
        dq = jnp.dot(score_grad, key_window, preferred_element_type=jnp.float32) * scale
        res_ref[0, :, width + head * HEAD_DIM : width + (head + 1) * HEAD_DIM] = dq.astype(
            jnp.bfloat16
        )
        dk = lax.dot_general(score_grad, query, TRANS_A, preferred_element_type=jnp.float32)
        dv = lax.dot_general(soft_low, grad, TRANS_A, preferred_element_type=jnp.float32)
        if dk_sum is None:
            dk_sum, dv_sum = dk, dv
        else:
            dk_sum, dv_sum = dk_sum + dk, dv_sum + dv
    dk_ref[pl.ds(start, window_rows), :] += dk_sum * scale
    dv_ref[pl.ds(start, window_rows), :] += dv_sum


def fused_attention(slots, query_blocks, grad_blocks, halo_key, halo_value, halo_doc, slot_count):
    blocks, _, width = query_blocks.shape
    window_rows = BAND * BLOCK
    reach = (BAND - 1) * BLOCK
    halo_rows = halo_key.shape[0]
    query_doc = halo_doc[reach:].reshape(blocks, BLOCK, 1)
    key_doc = jnp.stack(
        [halo_doc[b * BLOCK : b * BLOCK + window_rows] for b in range(blocks)]
    ).reshape(blocks, 1, window_rows)
    block_spec = pl.BlockSpec((1, BLOCK, width), lambda b, slot: (b, 0, 0))
    whole = pl.BlockSpec((halo_rows, HEAD_DIM), lambda b, slot: (0, 0))
    grid_spec = pltpu.PrefetchScalarGridSpec(
        num_scalar_prefetch=1,
        grid=(blocks,),
        in_specs=[
            pl.BlockSpec((1, BLOCK, 1), lambda b, slot: (b, 0, 0)),
            pl.BlockSpec((1, 1, window_rows), lambda b, slot: (b, 0, 0)),
            block_spec,
            block_spec,
            whole,
            whole,
        ],
        out_specs=[
            pl.BlockSpec((1, BLOCK, 2 * width), lambda b, slot: (slot[b], 0, 0)),
            whole,
            whole,
        ],
    )
    return pl.pallas_call(
        fused_kernel,
        grid_spec=grid_spec,
        out_shape=[
            jax.ShapeDtypeStruct((slot_count, BLOCK, 2 * width), jnp.bfloat16),
            jax.ShapeDtypeStruct((halo_rows, HEAD_DIM), jnp.float32),
            jax.ShapeDtypeStruct((halo_rows, HEAD_DIM), jnp.float32),
        ],
        compiler_params=pltpu.CompilerParams(dimension_semantics=("arbitrary",)),
    )(slots, query_doc, key_doc, query_blocks, grad_blocks, halo_key, halo_value)


def shift_from_below(x, ctx_count, distance):
    pairs = [(s, s + distance) for s in range(ctx_count - distance)]
    return lax.ppermute(x, "ctx", pairs)


def shift_to_below(x, ctx_count, distance):
    pairs = [(s + distance, s) for s in range(ctx_count - distance)]
    return lax.ppermute(x, "ctx", pairs)


def on_device(queries, key_rows, value_rows, out_grad, doc_ids, block_owner):
    ctx_count = lax.axis_size("ctx")
    tp_count = lax.axis_size("tp")
    ctx_rank = lax.axis_index("ctx")
    local_rows, width = queries.shape
    head_cols = width // tp_count
    first_cols = (head_cols // HEAD_DIM) * FIRST_SHARE // 8 * HEAD_DIM
    bounds = [(0, first_cols), (first_cols, head_cols)]
    tok_dev = key_rows.shape[0]
    kv_cols = key_rows.shape[1]
    blocks_here = tok_dev // BLOCK
    reach = (BAND - 1) * BLOCK
    far = reach - tok_dev
    own_targets, held_sources = routing(block_owner, ctx_count, ctx_rank, blocks_here)
    kv_here = jnp.concatenate([key_rows, value_rows], axis=1)
    kv_near = shift_from_below(kv_here, ctx_count, 1)
    kv_far = shift_from_below(kv_here[tok_dev - far :], ctx_count, 2)
    halo = jnp.concatenate([kv_far, kv_near, kv_here], axis=0)
    halo_key = halo[:, :kv_cols]
    halo_value = halo[:, kv_cols:]
    padded_doc = jnp.concatenate([jnp.full((reach,), -1, doc_ids.dtype), doc_ids])
    halo_doc = lax.dynamic_slice_in_dim(padded_doc, ctx_rank * tok_dev, reach + tok_dev, 0)
    query_parts = queries.reshape(local_rows, tp_count, head_cols)
    grad_parts = out_grad.reshape(local_rows, tp_count, head_cols)
    held_parts = []
    key_grad = None
    for chunk, (low, high) in enumerate(bounds):
        chunk_cols = high - low
        both = jnp.concatenate([query_parts[:, :, low:high], grad_parts[:, :, low:high]], axis=-1)
        if chunk > 0:
            both, _ = lax.optimization_barrier((both, halo))
        both = lax.all_to_all(both, "tp", split_axis=1, concat_axis=0, tiled=True)
        both = both.reshape(blocks_here, BLOCK, 2 * chunk_cols)
        results, chunk_key_grad, chunk_value_grad = fused_attention(
            own_targets,
            both[..., :chunk_cols],
            both[..., chunk_cols:],
            halo_key,
            halo_value,
            halo_doc,
            ctx_count,
        )
        if key_grad is None:
            key_grad, value_grad = chunk_key_grad, chunk_value_grad
        else:
            key_grad = key_grad + chunk_key_grad
            value_grad = value_grad + chunk_value_grad
        sent = lax.all_to_all(results, "ctx", split_axis=0, concat_axis=0, tiled=True)
        held_parts.append(jnp.take(sent, held_sources, axis=0))
    kv_grad = jnp.concatenate([key_grad, value_grad], axis=1)
    grad_near = shift_to_below(kv_grad[far:reach].astype(jnp.bfloat16), ctx_count, 1)
    grad_far = shift_to_below(kv_grad[:far].astype(jnp.bfloat16), ctx_count, 2)
    kv_total = kv_grad[reach:] + grad_near.astype(jnp.float32)
    kv_total = kv_total.at[tok_dev - far :].add(grad_far.astype(jnp.float32))
    widths = [high - low for low, high in bounds]
    held_out = jnp.concatenate([p[..., :w] for p, w in zip(held_parts, widths)], axis=-1)
    held_dq = jnp.concatenate([p[..., w:] for p, w in zip(held_parts, widths)], axis=-1)
    return (
        held_out.reshape(tok_dev, head_cols),
        held_dq.reshape(tok_dev, head_cols),
        kv_total[:, :kv_cols].astype(jnp.bfloat16),
        kv_total[:, kv_cols:].astype(jnp.bfloat16),
    )


def solution(mesh):
    return jax.shard_map(
        on_device,
        mesh=mesh,
        in_specs=(
            P(("ctx", "tp"), None),
            P("ctx", "tp"),
            P("ctx", "tp"),
            P(("ctx", "tp"), None),
            P(),
            P(),
        ),
        out_specs=(P("ctx", "tp"), P("ctx", "tp"), P("ctx", "tp"), P("ctx", "tp")),
        check_vma=False,
    )
```

```python
import jax
import jax.numpy as jnp
from jax import lax
from jax.sharding import PartitionSpec as P
from jax.experimental import pallas as pl
from jax.experimental.pallas import tpu as pltpu

HEADS = 64
KV_HEADS = 8
HEAD_DIM = 128
BLOCK = 128
BAND = 12
FIRST_SHARE = 3


def routing(block_owner, ctx_count, ctx_rank, blocks_here):
    owner_grid = block_owner.reshape(ctx_count, blocks_here)
    own_targets = lax.dynamic_index_in_dim(owner_grid, ctx_rank, 0, keepdims=False)
    sources = jnp.arange(ctx_count, dtype=jnp.int32)
    present = jnp.sum((owner_grid == ctx_rank).astype(jnp.int32), axis=1)
    arrival_rank = jnp.cumsum(present) - 1
    slot_index = jnp.arange(blocks_here, dtype=jnp.int32)
    chosen = (present[None, :] == 1) & (arrival_rank[None, :] == slot_index[:, None])
    held_sources = jnp.sum(chosen.astype(jnp.int32) * sources[None, :], axis=1)
    return (own_targets, held_sources)


def select_rows(selector, blocks):
    picked = jnp.einsum("ab,brh->arh", selector, blocks, preferred_element_type=jnp.float32)
    return picked.astype(jnp.bfloat16)


def halo_docs(doc_ids, first_row, halo_rows):
    positions = first_row + jnp.arange(halo_rows, dtype=jnp.int32)
    picked = jnp.take(doc_ids, jnp.clip(positions, 0, doc_ids.shape[0] - 1), axis=0)
    return jnp.where(positions >= 0, picked, -1)


def masked_scores(query_block, key_window, query_doc, key_doc, local_block):
    window_rows = key_window.shape[0]
    kv_local = key_window.shape[1]
    query_heads = query_block.reshape(BLOCK, kv_local, HEADS // KV_HEADS, HEAD_DIM)
    raw_scores = jnp.einsum(
        "qkgd,wkd->kgqw", query_heads, key_window, preferred_element_type=jnp.float32
    ) * HEAD_DIM ** (-0.5)
    query_pos = (BAND - 1) * BLOCK + jnp.arange(BLOCK, dtype=jnp.int32)
    key_pos = jnp.arange(window_rows, dtype=jnp.int32)
    allowed = (query_doc[:, None] == key_doc[None, :]) & (key_pos[None, :] <= query_pos[:, None])
    return (jnp.where(allowed[None, None], raw_scores, -1e30), query_heads)


def window_of(halo_key, halo_value, halo_doc, local_block):
    window_rows = BAND * BLOCK
    kv_local = halo_key.shape[1] // HEAD_DIM
    start = local_block * BLOCK
    key_window = lax.dynamic_slice_in_dim(halo_key, start, window_rows, 0)
    value_window = lax.dynamic_slice_in_dim(halo_value, start, window_rows, 0)
    key_doc = lax.dynamic_slice_in_dim(halo_doc, start, window_rows, 0)
    query_doc = lax.dynamic_slice_in_dim(halo_doc, start + (BAND - 1) * BLOCK, BLOCK, 0)
    return (
        key_window.reshape(window_rows, kv_local, HEAD_DIM),
        value_window.reshape(window_rows, kv_local, HEAD_DIM),
        query_doc,
        key_doc,
    )


def attend_forward(query_blocks, halo_key, halo_value, halo_doc):

    def advance(running, inputs):
        query_block, local_block = inputs
        key_window, value_window, query_doc, key_doc = window_of(
            halo_key, halo_value, halo_doc, local_block
        )
        scores, _ = masked_scores(query_block, key_window, query_doc, key_doc, local_block)
        row_max = jnp.max(scores, axis=-1, keepdims=True)
        log_total = row_max + jnp.log(jnp.sum(jnp.exp(scores - row_max), axis=-1, keepdims=True))
        soft_low = jnp.exp(scores - log_total).astype(jnp.bfloat16)
        natural_out = jnp.einsum(
            "kgqw,wkd->qkgd", soft_low, value_window, preferred_element_type=jnp.float32
        )
        return (running, (natural_out.reshape(BLOCK, -1).astype(jnp.bfloat16), log_total))

    local_ids = jnp.arange(query_blocks.shape[0], dtype=jnp.int32)
    _, (out_blocks, log_totals) = lax.scan(
        advance, jnp.zeros((), jnp.float32), (query_blocks, local_ids)
    )
    return (out_blocks, log_totals)


def attend_backward(query_blocks, grad_blocks, out_blocks, log_totals, halo_key, halo_value, halo_doc):
    window_rows = BAND * BLOCK
    inv_root = HEAD_DIM ** (-0.5)

    def advance(running, inputs):
        key_grad, value_grad = running
        query_block, grad_block, out_block, log_total, local_block = inputs
        key_window, value_window, query_doc, key_doc = window_of(
            halo_key, halo_value, halo_doc, local_block
        )
        scores, query_heads = masked_scores(
            query_block, key_window, query_doc, key_doc, local_block
        )
        grad_heads = grad_block.reshape(query_heads.shape)
        out_heads = out_block.reshape(query_heads.shape)
        weights = jnp.exp(scores - log_total)
        soft_low = weights.astype(jnp.bfloat16)
        row_dot = jnp.sum(grad_heads.astype(jnp.float32) * out_heads.astype(jnp.float32), axis=-1)
        row_dot = jnp.transpose(row_dot, (1, 2, 0))[..., None]
        prob_grad = jnp.einsum(
            "qkgd,wkd->kgqw", grad_heads, value_window, preferred_element_type=jnp.float32
        )
        score_grad = (weights * (prob_grad - row_dot)).astype(jnp.bfloat16)
        query_part = (
            jnp.einsum("kgqw,wkd->qkgd", score_grad, key_window, preferred_element_type=jnp.float32)
            * inv_root
        )
        key_part = (
            jnp.einsum(
                "kgqw,qkgd->wkd", score_grad, query_heads, preferred_element_type=jnp.float32
            )
            * inv_root
        )
        value_part = jnp.einsum(
            "kgqw,qkgd->wkd", soft_low, grad_heads, preferred_element_type=jnp.float32
        )
        start = local_block * BLOCK
        old_keys = lax.dynamic_slice_in_dim(key_grad, start, window_rows, 0)
        old_values = lax.dynamic_slice_in_dim(value_grad, start, window_rows, 0)
        key_grad = lax.dynamic_update_slice_in_dim(
            key_grad, old_keys + key_part.reshape(window_rows, -1), start, 0
        )
        value_grad = lax.dynamic_update_slice_in_dim(
            value_grad, old_values + value_part.reshape(window_rows, -1), start, 0
        )
        return ((key_grad, value_grad), query_part.reshape(BLOCK, -1).astype(jnp.bfloat16))

    zero_grads = (
        jnp.zeros(halo_key.shape, jnp.float32),
        jnp.zeros(halo_value.shape, jnp.float32),
    )
    local_ids = jnp.arange(query_blocks.shape[0], dtype=jnp.int32)
    (key_grad, value_grad), dq_blocks = lax.scan(
        advance, zero_grads, (query_blocks, grad_blocks, out_blocks, log_totals, local_ids)
    )
    return (dq_blocks, key_grad, value_grad)


TRANS_B = (((1,), (1,)), ((), ()))
TRANS_A = (((0,), (0,)), ((), ()))


def fused_kernel(slot_ref, qdoc_ref, kdoc_ref, q_ref, do_ref, k_ref, v_ref, res_ref, dk_ref, dv_ref):
    block = pl.program_id(0)
    window_rows = BAND * BLOCK
    scale = HEAD_DIM ** (-0.5)
    width = q_ref.shape[2]
    heads_here = width // HEAD_DIM

    @pl.when(block == 0)
    def _():
        dk_ref[...] = jnp.zeros_like(dk_ref)
        dv_ref[...] = jnp.zeros_like(dv_ref)

    start = pl.multiple_of(block * BLOCK, BLOCK)
    key_window = k_ref[pl.ds(start, window_rows), :]
    value_window = v_ref[pl.ds(start, window_rows), :]
    shape = (BLOCK, window_rows)
    rows = lax.broadcasted_iota(jnp.int32, shape, 0) + (BAND - 1) * BLOCK
    cols = lax.broadcasted_iota(jnp.int32, shape, 1)
    allowed = (qdoc_ref[0] == kdoc_ref[0]) & (cols <= rows)
    bias = jnp.where(allowed, 0.0, -1e30).astype(jnp.float32)
    dk_sum = None
    for head in range(heads_here):
        cols_of = slice(head * HEAD_DIM, (head + 1) * HEAD_DIM)
        query = q_ref[0, :, cols_of]
        raw = lax.dot_general(query, key_window, TRANS_B, preferred_element_type=jnp.float32) * scale
        scores = raw + bias
        row_max = jnp.max(scores, axis=1, keepdims=True)
        shifted = jnp.exp(scores - row_max)
        weights = shifted * (1.0 / jnp.sum(shifted, axis=1, keepdims=True))
        soft_low = weights.astype(jnp.bfloat16)
        out = jnp.dot(soft_low, value_window, preferred_element_type=jnp.float32).astype(jnp.bfloat16)
        res_ref[0, :, cols_of] = out
        grad = do_ref[0, :, cols_of]
        row_dot = jnp.sum(grad.astype(jnp.float32) * out.astype(jnp.float32), axis=1, keepdims=True)
        prob_grad = lax.dot_general(grad, value_window, TRANS_B, preferred_element_type=jnp.float32)
        score_grad = (weights * (prob_grad - row_dot)).astype(jnp.bfloat16)
        dq = jnp.dot(score_grad, key_window, preferred_element_type=jnp.float32) * scale
        res_ref[0, :, width + head * HEAD_DIM : width + (head + 1) * HEAD_DIM] = dq.astype(
            jnp.bfloat16
        )
        dk = lax.dot_general(score_grad, query, TRANS_A, preferred_element_type=jnp.float32)
        dv = lax.dot_general(soft_low, grad, TRANS_A, preferred_element_type=jnp.float32)
        if dk_sum is None:
            dk_sum, dv_sum = dk, dv
        else:
            dk_sum, dv_sum = dk_sum + dk, dv_sum + dv
    dk_ref[pl.ds(start, window_rows), :] += dk_sum * scale
    dv_ref[pl.ds(start, window_rows), :] += dv_sum


def fused_attention(slots, query_blocks, grad_blocks, halo_key, halo_value, halo_doc, slot_count):
    blocks, _, width = query_blocks.shape
    window_rows = BAND * BLOCK
    reach = (BAND - 1) * BLOCK
    halo_rows = halo_key.shape[0]
    query_doc = halo_doc[reach:].reshape(blocks, BLOCK, 1)
    key_doc = jnp.stack(
        [halo_doc[b * BLOCK : b * BLOCK + window_rows] for b in range(blocks)]
    ).reshape(blocks, 1, window_rows)
    block_spec = pl.BlockSpec((1, BLOCK, width), lambda b, slot: (b, 0, 0))
    whole = pl.BlockSpec((halo_rows, HEAD_DIM), lambda b, slot: (0, 0))
    grid_spec = pltpu.PrefetchScalarGridSpec(
        num_scalar_prefetch=1,
        grid=(blocks,),
        in_specs=[
            pl.BlockSpec((1, BLOCK, 1), lambda b, slot: (b, 0, 0)),
            pl.BlockSpec((1, 1, window_rows), lambda b, slot: (b, 0, 0)),
            block_spec,
            block_spec,
            whole,
            whole,
        ],
        out_specs=[
            pl.BlockSpec((1, BLOCK, 2 * width), lambda b, slot: (slot[b], 0, 0)),
            whole,
            whole,
        ],
    )
    return pl.pallas_call(
        fused_kernel,
        grid_spec=grid_spec,
        out_shape=[
            jax.ShapeDtypeStruct((slot_count, BLOCK, 2 * width), jnp.bfloat16),
            jax.ShapeDtypeStruct((halo_rows, HEAD_DIM), jnp.float32),
            jax.ShapeDtypeStruct((halo_rows, HEAD_DIM), jnp.float32),
        ],
        compiler_params=pltpu.CompilerParams(dimension_semantics=("arbitrary",)),
    )(slots, query_doc, key_doc, query_blocks, grad_blocks, halo_key, halo_value)


def shift_from_below(x, ctx_count, distance):
    pairs = [(s, s + distance) for s in range(ctx_count - distance)]
    return lax.ppermute(x, "ctx", pairs)


def shift_to_below(x, ctx_count, distance):
    pairs = [(s + distance, s) for s in range(ctx_count - distance)]
    return lax.ppermute(x, "ctx", pairs)


def on_device(queries, key_rows, value_rows, out_grad, doc_ids, block_owner):
    ctx_count = lax.axis_size("ctx")
    tp_count = lax.axis_size("tp")
    ctx_rank = lax.axis_index("ctx")
    local_rows, width = queries.shape
    head_cols = width // tp_count
    first_cols = (head_cols // HEAD_DIM) * FIRST_SHARE // 8 * HEAD_DIM
    bounds = [(0, first_cols), (first_cols, head_cols)]
    tok_dev = key_rows.shape[0]
    kv_cols = key_rows.shape[1]
    blocks_here = tok_dev // BLOCK
    reach = (BAND - 1) * BLOCK
    far = reach - tok_dev
    own_targets, held_sources = routing(block_owner, ctx_count, ctx_rank, blocks_here)
    kv_here = jnp.concatenate([key_rows, value_rows], axis=1)
    kv_near = shift_from_below(kv_here, ctx_count, 1)
    kv_far = shift_from_below(kv_here[tok_dev - far :], ctx_count, 2)
    halo = jnp.concatenate([kv_far, kv_near, kv_here], axis=0)
    halo_key = halo[:, :kv_cols]
    halo_value = halo[:, kv_cols:]
    padded_doc = jnp.concatenate([jnp.full((reach,), -1, doc_ids.dtype), doc_ids])
    halo_doc = lax.dynamic_slice_in_dim(padded_doc, ctx_rank * tok_dev, reach + tok_dev, 0)
    query_parts = queries.reshape(local_rows, tp_count, head_cols)
    grad_parts = out_grad.reshape(local_rows, tp_count, head_cols)
    held_parts = []
    key_grad = None
    for chunk, (low, high) in enumerate(bounds):
        chunk_cols = high - low
        both = jnp.concatenate([query_parts[:, :, low:high], grad_parts[:, :, low:high]], axis=-1)
        if chunk > 0:
            both, _ = lax.optimization_barrier((both, halo))
        both = lax.all_to_all(both, "tp", split_axis=1, concat_axis=0, tiled=True)
        both = both.reshape(blocks_here, BLOCK, 2 * chunk_cols)
        results, chunk_key_grad, chunk_value_grad = fused_attention(
            own_targets,
            both[..., :chunk_cols],
            both[..., chunk_cols:],
            halo_key,
            halo_value,
            halo_doc,
            ctx_count,
        )
        if key_grad is None:
            key_grad, value_grad = chunk_key_grad, chunk_value_grad
        else:
            key_grad = key_grad + chunk_key_grad
            value_grad = value_grad + chunk_value_grad
        if chunk == len(bounds) - 1:
            kv_grad = jnp.concatenate([key_grad, value_grad], axis=1)
            grad_near = shift_to_below(kv_grad[far:reach].astype(jnp.bfloat16), ctx_count, 1)
            grad_far = shift_to_below(kv_grad[:far].astype(jnp.bfloat16), ctx_count, 2)
            results, grad_near, grad_far = lax.optimization_barrier((results, grad_near, grad_far))
        sent = lax.all_to_all(results, "ctx", split_axis=0, concat_axis=0, tiled=True)
        held_parts.append(jnp.take(sent, held_sources, axis=0))
    kv_total = kv_grad[reach:] + grad_near.astype(jnp.float32)
    kv_total = kv_total.at[tok_dev - far :].add(grad_far.astype(jnp.float32))
    widths = [high - low for low, high in bounds]
    held_out = jnp.concatenate([p[..., :w] for p, w in zip(held_parts, widths)], axis=-1)
    held_dq = jnp.concatenate([p[..., w:] for p, w in zip(held_parts, widths)], axis=-1)
    return (
        held_out.reshape(tok_dev, head_cols),
        held_dq.reshape(tok_dev, head_cols),
        kv_total[:, :kv_cols].astype(jnp.bfloat16),
        kv_total[:, kv_cols:].astype(jnp.bfloat16),
    )


def solution(mesh):
    return jax.shard_map(
        on_device,
        mesh=mesh,
        in_specs=(
            P(("ctx", "tp"), None),
            P("ctx", "tp"),
            P("ctx", "tp"),
            P(("ctx", "tp"), None),
            P(),
            P(),
        ),
        out_specs=(P("ctx", "tp"), P("ctx", "tp"), P("ctx", "tp"), P("ctx", "tp")),
        check_vma=False,
    )
```

```python
import jax
import jax.numpy as jnp
from jax import lax
from jax.sharding import PartitionSpec as P
from jax.experimental import pallas as pl
from jax.experimental.pallas import tpu as pltpu

HEADS = 64
KV_HEADS = 8
HEAD_DIM = 128
BLOCK = 128
BAND = 12
FIRST_SHARE = 2


def routing(block_owner, ctx_count, ctx_rank, blocks_here):
    owner_grid = block_owner.reshape(ctx_count, blocks_here)
    own_targets = lax.dynamic_index_in_dim(owner_grid, ctx_rank, 0, keepdims=False)
    sources = jnp.arange(ctx_count, dtype=jnp.int32)
    present = jnp.sum((owner_grid == ctx_rank).astype(jnp.int32), axis=1)
    arrival_rank = jnp.cumsum(present) - 1
    slot_index = jnp.arange(blocks_here, dtype=jnp.int32)
    chosen = (present[None, :] == 1) & (arrival_rank[None, :] == slot_index[:, None])
    held_sources = jnp.sum(chosen.astype(jnp.int32) * sources[None, :], axis=1)
    return (own_targets, held_sources)


def select_rows(selector, blocks):
    picked = jnp.einsum("ab,brh->arh", selector, blocks, preferred_element_type=jnp.float32)
    return picked.astype(jnp.bfloat16)


def halo_docs(doc_ids, first_row, halo_rows):
    positions = first_row + jnp.arange(halo_rows, dtype=jnp.int32)
    picked = jnp.take(doc_ids, jnp.clip(positions, 0, doc_ids.shape[0] - 1), axis=0)
    return jnp.where(positions >= 0, picked, -1)


def masked_scores(query_block, key_window, query_doc, key_doc, local_block):
    window_rows = key_window.shape[0]
    kv_local = key_window.shape[1]
    query_heads = query_block.reshape(BLOCK, kv_local, HEADS // KV_HEADS, HEAD_DIM)
    raw_scores = jnp.einsum(
        "qkgd,wkd->kgqw", query_heads, key_window, preferred_element_type=jnp.float32
    ) * HEAD_DIM ** (-0.5)
    query_pos = (BAND - 1) * BLOCK + jnp.arange(BLOCK, dtype=jnp.int32)
    key_pos = jnp.arange(window_rows, dtype=jnp.int32)
    allowed = (query_doc[:, None] == key_doc[None, :]) & (key_pos[None, :] <= query_pos[:, None])
    return (jnp.where(allowed[None, None], raw_scores, -1e30), query_heads)


def window_of(halo_key, halo_value, halo_doc, local_block):
    window_rows = BAND * BLOCK
    kv_local = halo_key.shape[1] // HEAD_DIM
    start = local_block * BLOCK
    key_window = lax.dynamic_slice_in_dim(halo_key, start, window_rows, 0)
    value_window = lax.dynamic_slice_in_dim(halo_value, start, window_rows, 0)
    key_doc = lax.dynamic_slice_in_dim(halo_doc, start, window_rows, 0)
    query_doc = lax.dynamic_slice_in_dim(halo_doc, start + (BAND - 1) * BLOCK, BLOCK, 0)
    return (
        key_window.reshape(window_rows, kv_local, HEAD_DIM),
        value_window.reshape(window_rows, kv_local, HEAD_DIM),
        query_doc,
        key_doc,
    )


def attend_forward(query_blocks, halo_key, halo_value, halo_doc):

    def advance(running, inputs):
        query_block, local_block = inputs
        key_window, value_window, query_doc, key_doc = window_of(
            halo_key, halo_value, halo_doc, local_block
        )
        scores, _ = masked_scores(query_block, key_window, query_doc, key_doc, local_block)
        row_max = jnp.max(scores, axis=-1, keepdims=True)
        log_total = row_max + jnp.log(jnp.sum(jnp.exp(scores - row_max), axis=-1, keepdims=True))
        soft_low = jnp.exp(scores - log_total).astype(jnp.bfloat16)
        natural_out = jnp.einsum(
            "kgqw,wkd->qkgd", soft_low, value_window, preferred_element_type=jnp.float32
        )
        return (running, (natural_out.reshape(BLOCK, -1).astype(jnp.bfloat16), log_total))

    local_ids = jnp.arange(query_blocks.shape[0], dtype=jnp.int32)
    _, (out_blocks, log_totals) = lax.scan(
        advance, jnp.zeros((), jnp.float32), (query_blocks, local_ids)
    )
    return (out_blocks, log_totals)


def attend_backward(query_blocks, grad_blocks, out_blocks, log_totals, halo_key, halo_value, halo_doc):
    window_rows = BAND * BLOCK
    inv_root = HEAD_DIM ** (-0.5)

    def advance(running, inputs):
        key_grad, value_grad = running
        query_block, grad_block, out_block, log_total, local_block = inputs
        key_window, value_window, query_doc, key_doc = window_of(
            halo_key, halo_value, halo_doc, local_block
        )
        scores, query_heads = masked_scores(
            query_block, key_window, query_doc, key_doc, local_block
        )
        grad_heads = grad_block.reshape(query_heads.shape)
        out_heads = out_block.reshape(query_heads.shape)
        weights = jnp.exp(scores - log_total)
        soft_low = weights.astype(jnp.bfloat16)
        row_dot = jnp.sum(grad_heads.astype(jnp.float32) * out_heads.astype(jnp.float32), axis=-1)
        row_dot = jnp.transpose(row_dot, (1, 2, 0))[..., None]
        prob_grad = jnp.einsum(
            "qkgd,wkd->kgqw", grad_heads, value_window, preferred_element_type=jnp.float32
        )
        score_grad = (weights * (prob_grad - row_dot)).astype(jnp.bfloat16)
        query_part = (
            jnp.einsum("kgqw,wkd->qkgd", score_grad, key_window, preferred_element_type=jnp.float32)
            * inv_root
        )
        key_part = (
            jnp.einsum(
                "kgqw,qkgd->wkd", score_grad, query_heads, preferred_element_type=jnp.float32
            )
            * inv_root
        )
        value_part = jnp.einsum(
            "kgqw,qkgd->wkd", soft_low, grad_heads, preferred_element_type=jnp.float32
        )
        start = local_block * BLOCK
        old_keys = lax.dynamic_slice_in_dim(key_grad, start, window_rows, 0)
        old_values = lax.dynamic_slice_in_dim(value_grad, start, window_rows, 0)
        key_grad = lax.dynamic_update_slice_in_dim(
            key_grad, old_keys + key_part.reshape(window_rows, -1), start, 0
        )
        value_grad = lax.dynamic_update_slice_in_dim(
            value_grad, old_values + value_part.reshape(window_rows, -1), start, 0
        )
        return ((key_grad, value_grad), query_part.reshape(BLOCK, -1).astype(jnp.bfloat16))

    zero_grads = (
        jnp.zeros(halo_key.shape, jnp.float32),
        jnp.zeros(halo_value.shape, jnp.float32),
    )
    local_ids = jnp.arange(query_blocks.shape[0], dtype=jnp.int32)
    (key_grad, value_grad), dq_blocks = lax.scan(
        advance, zero_grads, (query_blocks, grad_blocks, out_blocks, log_totals, local_ids)
    )
    return (dq_blocks, key_grad, value_grad)


TRANS_B = (((1,), (1,)), ((), ()))
TRANS_A = (((0,), (0,)), ((), ()))


def fused_kernel(slot_ref, qdoc_ref, kdoc_ref, q_ref, do_ref, k_ref, v_ref, res_ref, dk_ref, dv_ref):
    block = pl.program_id(0)
    window_rows = BAND * BLOCK
    scale = HEAD_DIM ** (-0.5)
    width = q_ref.shape[2]
    heads_here = width // HEAD_DIM

    @pl.when(block == 0)
    def _():
        dk_ref[...] = jnp.zeros_like(dk_ref)
        dv_ref[...] = jnp.zeros_like(dv_ref)

    start = pl.multiple_of(block * BLOCK, BLOCK)
    key_window = k_ref[pl.ds(start, window_rows), :]
    value_window = v_ref[pl.ds(start, window_rows), :]
    shape = (BLOCK, window_rows)
    rows = lax.broadcasted_iota(jnp.int32, shape, 0) + (BAND - 1) * BLOCK
    cols = lax.broadcasted_iota(jnp.int32, shape, 1)
    allowed = (qdoc_ref[0] == kdoc_ref[0]) & (cols <= rows)
    bias = jnp.where(allowed, 0.0, -1e30).astype(jnp.float32)
    dk_sum = None
    for head in range(heads_here):
        cols_of = slice(head * HEAD_DIM, (head + 1) * HEAD_DIM)
        query = q_ref[0, :, cols_of]
        raw = lax.dot_general(query, key_window, TRANS_B, preferred_element_type=jnp.float32) * scale
        scores = raw + bias
        row_max = jnp.max(scores, axis=1, keepdims=True)
        shifted = jnp.exp(scores - row_max)
        weights = shifted * (1.0 / jnp.sum(shifted, axis=1, keepdims=True))
        soft_low = weights.astype(jnp.bfloat16)
        out = jnp.dot(soft_low, value_window, preferred_element_type=jnp.float32).astype(jnp.bfloat16)
        res_ref[0, :, cols_of] = out
        grad = do_ref[0, :, cols_of]
        row_dot = jnp.sum(grad.astype(jnp.float32) * out.astype(jnp.float32), axis=1, keepdims=True)
        prob_grad = lax.dot_general(grad, value_window, TRANS_B, preferred_element_type=jnp.float32)
        score_grad = (weights * (prob_grad - row_dot)).astype(jnp.bfloat16)
        dq = jnp.dot(score_grad, key_window, preferred_element_type=jnp.float32) * scale
        res_ref[0, :, width + head * HEAD_DIM : width + (head + 1) * HEAD_DIM] = dq.astype(
            jnp.bfloat16
        )
        dk = lax.dot_general(score_grad, query, TRANS_A, preferred_element_type=jnp.float32)
        dv = lax.dot_general(soft_low, grad, TRANS_A, preferred_element_type=jnp.float32)
        if dk_sum is None:
            dk_sum, dv_sum = dk, dv
        else:
            dk_sum, dv_sum = dk_sum + dk, dv_sum + dv
    dk_ref[pl.ds(start, window_rows), :] += dk_sum * scale
    dv_ref[pl.ds(start, window_rows), :] += dv_sum


def fused_attention(slots, query_blocks, grad_blocks, halo_key, halo_value, halo_doc, slot_count):
    blocks, _, width = query_blocks.shape
    window_rows = BAND * BLOCK
    reach = (BAND - 1) * BLOCK
    halo_rows = halo_key.shape[0]
    query_doc = halo_doc[reach:].reshape(blocks, BLOCK, 1)
    key_doc = jnp.stack(
        [halo_doc[b * BLOCK : b * BLOCK + window_rows] for b in range(blocks)]
    ).reshape(blocks, 1, window_rows)
    block_spec = pl.BlockSpec((1, BLOCK, width), lambda b, slot: (b, 0, 0))
    whole = pl.BlockSpec((halo_rows, HEAD_DIM), lambda b, slot: (0, 0))
    grid_spec = pltpu.PrefetchScalarGridSpec(
        num_scalar_prefetch=1,
        grid=(blocks,),
        in_specs=[
            pl.BlockSpec((1, BLOCK, 1), lambda b, slot: (b, 0, 0)),
            pl.BlockSpec((1, 1, window_rows), lambda b, slot: (b, 0, 0)),
            block_spec,
            block_spec,
            whole,
            whole,
        ],
        out_specs=[
            pl.BlockSpec((1, BLOCK, 2 * width), lambda b, slot: (slot[b], 0, 0)),
            whole,
            whole,
        ],
    )
    return pl.pallas_call(
        fused_kernel,
        grid_spec=grid_spec,
        out_shape=[
            jax.ShapeDtypeStruct((slot_count, BLOCK, 2 * width), jnp.bfloat16),
            jax.ShapeDtypeStruct((halo_rows, HEAD_DIM), jnp.float32),
            jax.ShapeDtypeStruct((halo_rows, HEAD_DIM), jnp.float32),
        ],
        compiler_params=pltpu.CompilerParams(dimension_semantics=("arbitrary",)),
    )(slots, query_doc, key_doc, query_blocks, grad_blocks, halo_key, halo_value)


def shift_from_below(x, ctx_count, distance):
    pairs = [(s, s + distance) for s in range(ctx_count - distance)]
    return lax.ppermute(x, "ctx", pairs)


def shift_to_below(x, ctx_count, distance):
    pairs = [(s + distance, s) for s in range(ctx_count - distance)]
    return lax.ppermute(x, "ctx", pairs)


def on_device(queries, key_rows, value_rows, out_grad, doc_ids, block_owner):
    ctx_count = lax.axis_size("ctx")
    tp_count = lax.axis_size("tp")
    ctx_rank = lax.axis_index("ctx")
    local_rows, width = queries.shape
    head_cols = width // tp_count
    first_cols = (head_cols // HEAD_DIM) * FIRST_SHARE // 8 * HEAD_DIM
    bounds = [(0, first_cols), (first_cols, head_cols)]
    tok_dev = key_rows.shape[0]
    kv_cols = key_rows.shape[1]
    blocks_here = tok_dev // BLOCK
    reach = (BAND - 1) * BLOCK
    far = reach - tok_dev
    own_targets, held_sources = routing(block_owner, ctx_count, ctx_rank, blocks_here)
    kv_here = jnp.concatenate([key_rows, value_rows], axis=1)
    kv_near = shift_from_below(kv_here, ctx_count, 1)
    kv_far = shift_from_below(kv_here[tok_dev - far :], ctx_count, 2)
    halo = jnp.concatenate([kv_far, kv_near, kv_here], axis=0)
    halo_key = halo[:, :kv_cols]
    halo_value = halo[:, kv_cols:]
    padded_doc = jnp.concatenate([jnp.full((reach,), -1, doc_ids.dtype), doc_ids])
    halo_doc = lax.dynamic_slice_in_dim(padded_doc, ctx_rank * tok_dev, reach + tok_dev, 0)
    query_parts = queries.reshape(local_rows, tp_count, head_cols)
    grad_parts = out_grad.reshape(local_rows, tp_count, head_cols)
    held_parts = []
    key_grad = None
    for chunk, (low, high) in enumerate(bounds):
        chunk_cols = high - low
        both = jnp.concatenate([query_parts[:, :, low:high], grad_parts[:, :, low:high]], axis=-1)
        if chunk > 0:
            both, _ = lax.optimization_barrier((both, halo))
        both = lax.all_to_all(both, "tp", split_axis=1, concat_axis=0, tiled=True)
        both = both.reshape(blocks_here, BLOCK, 2 * chunk_cols)
        results, chunk_key_grad, chunk_value_grad = fused_attention(
            own_targets,
            both[..., :chunk_cols],
            both[..., chunk_cols:],
            halo_key,
            halo_value,
            halo_doc,
            ctx_count,
        )
        if key_grad is None:
            key_grad, value_grad = chunk_key_grad, chunk_value_grad
        else:
            key_grad = key_grad + chunk_key_grad
            value_grad = value_grad + chunk_value_grad
        sent = lax.all_to_all(results, "ctx", split_axis=0, concat_axis=0, tiled=True)
        held_parts.append(jnp.take(sent, held_sources, axis=0))
    kv_grad = jnp.concatenate([key_grad, value_grad], axis=1)
    grad_near = shift_to_below(kv_grad[far:reach].astype(jnp.bfloat16), ctx_count, 1)
    grad_far = shift_to_below(kv_grad[:far].astype(jnp.bfloat16), ctx_count, 2)
    kv_total = kv_grad[reach:] + grad_near.astype(jnp.float32)
    kv_total = kv_total.at[tok_dev - far :].add(grad_far.astype(jnp.float32))
    widths = [high - low for low, high in bounds]
    held_out = jnp.concatenate([p[..., :w] for p, w in zip(held_parts, widths)], axis=-1)
    held_dq = jnp.concatenate([p[..., w:] for p, w in zip(held_parts, widths)], axis=-1)
    return (
        held_out.reshape(tok_dev, head_cols),
        held_dq.reshape(tok_dev, head_cols),
        kv_total[:, :kv_cols].astype(jnp.bfloat16),
        kv_total[:, kv_cols:].astype(jnp.bfloat16),
    )


def solution(mesh):
    return jax.shard_map(
        on_device,
        mesh=mesh,
        in_specs=(
            P(("ctx", "tp"), None),
            P("ctx", "tp"),
            P("ctx", "tp"),
            P(("ctx", "tp"), None),
            P(),
            P(),
        ),
        out_specs=(P("ctx", "tp"), P("ctx", "tp"), P("ctx", "tp"), P("ctx", "tp")),
        check_vma=False,
    )
```

```python
import jax
import jax.numpy as jnp
from jax import lax
from jax.sharding import PartitionSpec as P
from jax.experimental import pallas as pl
from jax.experimental.pallas import tpu as pltpu

HEADS = 64
KV_HEADS = 8
HEAD_DIM = 128
BLOCK = 128
BAND = 12
FIRST_SHARE = 3


def routing(block_owner, ctx_count, ctx_rank, blocks_here):
    owner_grid = block_owner.reshape(ctx_count, blocks_here)
    own_targets = lax.dynamic_index_in_dim(owner_grid, ctx_rank, 0, keepdims=False)
    sources = jnp.arange(ctx_count, dtype=jnp.int32)
    present = jnp.sum((owner_grid == ctx_rank).astype(jnp.int32), axis=1)
    arrival_rank = jnp.cumsum(present) - 1
    slot_index = jnp.arange(blocks_here, dtype=jnp.int32)
    chosen = (present[None, :] == 1) & (arrival_rank[None, :] == slot_index[:, None])
    held_sources = jnp.sum(chosen.astype(jnp.int32) * sources[None, :], axis=1)
    return (own_targets, held_sources)


def select_rows(selector, blocks):
    picked = jnp.einsum("ab,brh->arh", selector, blocks, preferred_element_type=jnp.float32)
    return picked.astype(jnp.bfloat16)


def halo_docs(doc_ids, first_row, halo_rows):
    positions = first_row + jnp.arange(halo_rows, dtype=jnp.int32)
    picked = jnp.take(doc_ids, jnp.clip(positions, 0, doc_ids.shape[0] - 1), axis=0)
    return jnp.where(positions >= 0, picked, -1)


def masked_scores(query_block, key_window, query_doc, key_doc, local_block):
    window_rows = key_window.shape[0]
    kv_local = key_window.shape[1]
    query_heads = query_block.reshape(BLOCK, kv_local, HEADS // KV_HEADS, HEAD_DIM)
    raw_scores = jnp.einsum(
        "qkgd,wkd->kgqw", query_heads, key_window, preferred_element_type=jnp.float32
    ) * HEAD_DIM ** (-0.5)
    query_pos = (BAND - 1) * BLOCK + jnp.arange(BLOCK, dtype=jnp.int32)
    key_pos = jnp.arange(window_rows, dtype=jnp.int32)
    allowed = (query_doc[:, None] == key_doc[None, :]) & (key_pos[None, :] <= query_pos[:, None])
    return (jnp.where(allowed[None, None], raw_scores, -1e30), query_heads)


def window_of(halo_key, halo_value, halo_doc, local_block):
    window_rows = BAND * BLOCK
    kv_local = halo_key.shape[1] // HEAD_DIM
    start = local_block * BLOCK
    key_window = lax.dynamic_slice_in_dim(halo_key, start, window_rows, 0)
    value_window = lax.dynamic_slice_in_dim(halo_value, start, window_rows, 0)
    key_doc = lax.dynamic_slice_in_dim(halo_doc, start, window_rows, 0)
    query_doc = lax.dynamic_slice_in_dim(halo_doc, start + (BAND - 1) * BLOCK, BLOCK, 0)
    return (
        key_window.reshape(window_rows, kv_local, HEAD_DIM),
        value_window.reshape(window_rows, kv_local, HEAD_DIM),
        query_doc,
        key_doc,
    )


def attend_forward(query_blocks, halo_key, halo_value, halo_doc):

    def advance(running, inputs):
        query_block, local_block = inputs
        key_window, value_window, query_doc, key_doc = window_of(
            halo_key, halo_value, halo_doc, local_block
        )
        scores, _ = masked_scores(query_block, key_window, query_doc, key_doc, local_block)
        row_max = jnp.max(scores, axis=-1, keepdims=True)
        log_total = row_max + jnp.log(jnp.sum(jnp.exp(scores - row_max), axis=-1, keepdims=True))
        soft_low = jnp.exp(scores - log_total).astype(jnp.bfloat16)
        natural_out = jnp.einsum(
            "kgqw,wkd->qkgd", soft_low, value_window, preferred_element_type=jnp.float32
        )
        return (running, (natural_out.reshape(BLOCK, -1).astype(jnp.bfloat16), log_total))

    local_ids = jnp.arange(query_blocks.shape[0], dtype=jnp.int32)
    _, (out_blocks, log_totals) = lax.scan(
        advance, jnp.zeros((), jnp.float32), (query_blocks, local_ids)
    )
    return (out_blocks, log_totals)


def attend_backward(query_blocks, grad_blocks, out_blocks, log_totals, halo_key, halo_value, halo_doc):
    window_rows = BAND * BLOCK
    inv_root = HEAD_DIM ** (-0.5)

    def advance(running, inputs):
        key_grad, value_grad = running
        query_block, grad_block, out_block, log_total, local_block = inputs
        key_window, value_window, query_doc, key_doc = window_of(
            halo_key, halo_value, halo_doc, local_block
        )
        scores, query_heads = masked_scores(
            query_block, key_window, query_doc, key_doc, local_block
        )
        grad_heads = grad_block.reshape(query_heads.shape)
        out_heads = out_block.reshape(query_heads.shape)
        weights = jnp.exp(scores - log_total)
        soft_low = weights.astype(jnp.bfloat16)
        row_dot = jnp.sum(grad_heads.astype(jnp.float32) * out_heads.astype(jnp.float32), axis=-1)
        row_dot = jnp.transpose(row_dot, (1, 2, 0))[..., None]
        prob_grad = jnp.einsum(
            "qkgd,wkd->kgqw", grad_heads, value_window, preferred_element_type=jnp.float32
        )
        score_grad = (weights * (prob_grad - row_dot)).astype(jnp.bfloat16)
        query_part = (
            jnp.einsum("kgqw,wkd->qkgd", score_grad, key_window, preferred_element_type=jnp.float32)
            * inv_root
        )
        key_part = (
            jnp.einsum(
                "kgqw,qkgd->wkd", score_grad, query_heads, preferred_element_type=jnp.float32
            )
            * inv_root
        )
        value_part = jnp.einsum(
            "kgqw,qkgd->wkd", soft_low, grad_heads, preferred_element_type=jnp.float32
        )
        start = local_block * BLOCK
        old_keys = lax.dynamic_slice_in_dim(key_grad, start, window_rows, 0)
        old_values = lax.dynamic_slice_in_dim(value_grad, start, window_rows, 0)
        key_grad = lax.dynamic_update_slice_in_dim(
            key_grad, old_keys + key_part.reshape(window_rows, -1), start, 0
        )
        value_grad = lax.dynamic_update_slice_in_dim(
            value_grad, old_values + value_part.reshape(window_rows, -1), start, 0
        )
        return ((key_grad, value_grad), query_part.reshape(BLOCK, -1).astype(jnp.bfloat16))

    zero_grads = (
        jnp.zeros(halo_key.shape, jnp.float32),
        jnp.zeros(halo_value.shape, jnp.float32),
    )
    local_ids = jnp.arange(query_blocks.shape[0], dtype=jnp.int32)
    (key_grad, value_grad), dq_blocks = lax.scan(
        advance, zero_grads, (query_blocks, grad_blocks, out_blocks, log_totals, local_ids)
    )
    return (dq_blocks, key_grad, value_grad)


TRANS_B = (((1,), (1,)), ((), ()))
TRANS_A = (((0,), (0,)), ((), ()))


def fused_kernel(slot_ref, qdoc_ref, kdoc_ref, q_ref, do_ref, k_ref, v_ref, res_ref, dk_ref, dv_ref):
    block = pl.program_id(0)
    window_rows = BAND * BLOCK
    scale = HEAD_DIM ** (-0.5)
    width = q_ref.shape[2]
    heads_here = width // HEAD_DIM

    @pl.when(block == 0)
    def _():
        dk_ref[...] = jnp.zeros_like(dk_ref)
        dv_ref[...] = jnp.zeros_like(dv_ref)

    start = pl.multiple_of(block * BLOCK, BLOCK)
    key_window = k_ref[pl.ds(start, window_rows), :]
    value_window = v_ref[pl.ds(start, window_rows), :]
    shape = (BLOCK, window_rows)
    rows = lax.broadcasted_iota(jnp.int32, shape, 0) + (BAND - 1) * BLOCK
    cols = lax.broadcasted_iota(jnp.int32, shape, 1)
    allowed = (qdoc_ref[0] == kdoc_ref[0]) & (cols <= rows)
    bias = jnp.where(allowed, 0.0, -1e30).astype(jnp.float32)
    dk_sum = None
    for head in range(heads_here):
        cols_of = slice(head * HEAD_DIM, (head + 1) * HEAD_DIM)
        query = q_ref[0, :, cols_of]
        raw = lax.dot_general(query, key_window, TRANS_B, preferred_element_type=jnp.float32) * scale
        scores = raw + bias
        row_max = jnp.max(scores, axis=1, keepdims=True)
        shifted = jnp.exp(scores - row_max)
        weights = shifted * (1.0 / jnp.sum(shifted, axis=1, keepdims=True))
        soft_low = weights.astype(jnp.bfloat16)
        out = jnp.dot(soft_low, value_window, preferred_element_type=jnp.float32).astype(jnp.bfloat16)
        res_ref[0, :, cols_of] = out
        grad = do_ref[0, :, cols_of]
        row_dot = jnp.sum(grad.astype(jnp.float32) * out.astype(jnp.float32), axis=1, keepdims=True)
        prob_grad = lax.dot_general(grad, value_window, TRANS_B, preferred_element_type=jnp.float32)
        score_grad = (weights * (prob_grad - row_dot)).astype(jnp.bfloat16)
        dq = jnp.dot(score_grad, key_window, preferred_element_type=jnp.float32) * scale
        res_ref[0, :, width + head * HEAD_DIM : width + (head + 1) * HEAD_DIM] = dq.astype(
            jnp.bfloat16
        )
        dk = lax.dot_general(score_grad, query, TRANS_A, preferred_element_type=jnp.float32)
        dv = lax.dot_general(soft_low, grad, TRANS_A, preferred_element_type=jnp.float32)
        if dk_sum is None:
            dk_sum, dv_sum = dk, dv
        else:
            dk_sum, dv_sum = dk_sum + dk, dv_sum + dv
    dk_ref[pl.ds(start, window_rows), :] += dk_sum * scale
    dv_ref[pl.ds(start, window_rows), :] += dv_sum


def fused_attention(slots, both_blocks, halo_key, halo_value, halo_doc, slot_count):
    blocks, _, both_width = both_blocks.shape
    width = both_width // 2
    window_rows = BAND * BLOCK
    reach = (BAND - 1) * BLOCK
    halo_rows = halo_key.shape[0]
    query_doc = halo_doc[reach:].reshape(blocks, BLOCK, 1)
    key_doc = jnp.stack(
        [halo_doc[b * BLOCK : b * BLOCK + window_rows] for b in range(blocks)]
    ).reshape(blocks, 1, window_rows)
    query_spec = pl.BlockSpec((1, BLOCK, width), lambda b, slot: (b, 0, 0))
    grad_spec = pl.BlockSpec((1, BLOCK, width), lambda b, slot: (b, 0, 1))
    whole = pl.BlockSpec((halo_rows, HEAD_DIM), lambda b, slot: (0, 0))
    grid_spec = pltpu.PrefetchScalarGridSpec(
        num_scalar_prefetch=1,
        grid=(blocks,),
        in_specs=[
            pl.BlockSpec((1, BLOCK, 1), lambda b, slot: (b, 0, 0)),
            pl.BlockSpec((1, 1, window_rows), lambda b, slot: (b, 0, 0)),
            query_spec,
            grad_spec,
            whole,
            whole,
        ],
        out_specs=[
            pl.BlockSpec((1, BLOCK, 2 * width), lambda b, slot: (slot[b], 0, 0)),
            whole,
            whole,
        ],
    )
    return pl.pallas_call(
        fused_kernel,
        grid_spec=grid_spec,
        out_shape=[
            jax.ShapeDtypeStruct((slot_count, BLOCK, 2 * width), jnp.bfloat16),
            jax.ShapeDtypeStruct((halo_rows, HEAD_DIM), jnp.float32),
            jax.ShapeDtypeStruct((halo_rows, HEAD_DIM), jnp.float32),
        ],
        compiler_params=pltpu.CompilerParams(dimension_semantics=("arbitrary",)),
    )(slots, query_doc, key_doc, both_blocks, both_blocks, halo_key, halo_value)


def shift_from_below(x, ctx_count, distance):
    pairs = [(s, s + distance) for s in range(ctx_count - distance)]
    return lax.ppermute(x, "ctx", pairs)


def shift_to_below(x, ctx_count, distance):
    pairs = [(s + distance, s) for s in range(ctx_count - distance)]
    return lax.ppermute(x, "ctx", pairs)


def on_device(queries, key_rows, value_rows, out_grad, doc_ids, block_owner):
    ctx_count = lax.axis_size("ctx")
    tp_count = lax.axis_size("tp")
    ctx_rank = lax.axis_index("ctx")
    local_rows, width = queries.shape
    head_cols = width // tp_count
    first_cols = (head_cols // HEAD_DIM) * FIRST_SHARE // 8 * HEAD_DIM
    bounds = [(0, first_cols), (first_cols, head_cols)]
    tok_dev = key_rows.shape[0]
    kv_cols = key_rows.shape[1]
    blocks_here = tok_dev // BLOCK
    reach = (BAND - 1) * BLOCK
    far = reach - tok_dev
    own_targets, held_sources = routing(block_owner, ctx_count, ctx_rank, blocks_here)
    kv_here = jnp.concatenate([key_rows, value_rows], axis=1)
    kv_near = shift_from_below(kv_here, ctx_count, 1)
    kv_far = shift_from_below(kv_here[tok_dev - far :], ctx_count, 2)
    halo = jnp.concatenate([kv_far, kv_near, kv_here], axis=0)
    halo_key = halo[:, :kv_cols]
    halo_value = halo[:, kv_cols:]
    padded_doc = jnp.concatenate([jnp.full((reach,), -1, doc_ids.dtype), doc_ids])
    halo_doc = lax.dynamic_slice_in_dim(padded_doc, ctx_rank * tok_dev, reach + tok_dev, 0)
    query_parts = queries.reshape(local_rows, tp_count, head_cols)
    grad_parts = out_grad.reshape(local_rows, tp_count, head_cols)
    held_parts = []
    key_grad = None
    for chunk, (low, high) in enumerate(bounds):
        chunk_cols = high - low
        both = jnp.concatenate([query_parts[:, :, low:high], grad_parts[:, :, low:high]], axis=-1)
        if chunk > 0:
            both, _ = lax.optimization_barrier((both, halo))
        both = lax.all_to_all(both, "tp", split_axis=1, concat_axis=0, tiled=True)
        both = both.reshape(blocks_here, BLOCK, 2 * chunk_cols)
        results, chunk_key_grad, chunk_value_grad = fused_attention(
            own_targets,
            both,
            halo_key,
            halo_value,
            halo_doc,
            ctx_count,
        )
        if key_grad is None:
            key_grad, value_grad = chunk_key_grad, chunk_value_grad
        else:
            key_grad = key_grad + chunk_key_grad
            value_grad = value_grad + chunk_value_grad
        sent = lax.all_to_all(results, "ctx", split_axis=0, concat_axis=0, tiled=True)
        held_parts.append(jnp.take(sent, held_sources, axis=0))
    kv_grad = jnp.concatenate([key_grad, value_grad], axis=1)
    grad_near = shift_to_below(kv_grad[far:reach].astype(jnp.bfloat16), ctx_count, 1)
    grad_far = shift_to_below(kv_grad[:far].astype(jnp.bfloat16), ctx_count, 2)
    kv_total = kv_grad[reach:] + grad_near.astype(jnp.float32)
    kv_total = kv_total.at[tok_dev - far :].add(grad_far.astype(jnp.float32))
    widths = [high - low for low, high in bounds]
    held_out = jnp.concatenate([p[..., :w] for p, w in zip(held_parts, widths)], axis=-1)
    held_dq = jnp.concatenate([p[..., w:] for p, w in zip(held_parts, widths)], axis=-1)
    return (
        held_out.reshape(tok_dev, head_cols),
        held_dq.reshape(tok_dev, head_cols),
        kv_total[:, :kv_cols].astype(jnp.bfloat16),
        kv_total[:, kv_cols:].astype(jnp.bfloat16),
    )


def solution(mesh):
    return jax.shard_map(
        on_device,
        mesh=mesh,
        in_specs=(
            P(("ctx", "tp"), None),
            P("ctx", "tp"),
            P("ctx", "tp"),
            P(("ctx", "tp"), None),
            P(),
            P(),
        ),
        out_specs=(P("ctx", "tp"), P("ctx", "tp"), P("ctx", "tp"), P("ctx", "tp")),
        check_vma=False,
    )
```
